256 devices in a mesh: seq: 16 (over x_hi, z), row: 4 (over x_lo, core), col: 4 (over y).
Axes of the slice: x: 4 (x_hi: 2, x_lo: 2; x = x_hi * 2 + x_lo), y: 4, z: 8, core: 2. Of those that a mesh axis runs over, the one named last changes fastest.
Arguments:
- tokens: bfloat16 [8192, 4096], P(('seq', 'col'), 'row'), may hold values from -11 to 11
- w_query: bfloat16 [4096, 4096], P('row', 'col'), as said below
- w_key: bfloat16 [4096, 1024], P('row', 'col'), as said below
- w_value: bfloat16 [4096, 1024], P('row', 'col'), may hold values from -0.09375 to 0.09375
- w_output: bfloat16 [4096, 4096], P('col', 'row'), may hold values from -0.09375 to 0.09375
Outputs:
- attended: bfloat16 [8192, 4096], P(('seq', 'col'), 'row')
The draws below stay inside these ranges and needn't reach their ends.
Inputs may be any that keep to these rules, and one draw needn't show every extreme that they name: `w_query`: entries below 6 / sqrt(4096) in magnitude. `w_key`: entries below 8.4 / sqrt(4096) in magnitude.
All inputs are finite; a program needn't handle non-finite values.
Results may differ from the reference program's by a relative error of at most 0.025.
Values may be sent and summed in bfloat16 or wider, within the bound.
No kernel may reach another device: no remote copies, remote signals or barrier semaphores. Data moves between devices by JAX's collectives and lax.ppermute only.
A program may use at most 64 MiB of HBM per device.

```python
import math
import jax
import jax.numpy as jnp
from jax import lax

D = 4096
HEADS = 32
KV_HEADS = 8
HEAD_DIM = 128
SEQ_LEN = 8192


def draw_tokens(key, part):
    drawn = jnp.clip(jax.random.normal(jax.random.fold_in(key, 3), (SEQ_LEN, D), jnp.float32), -6.0, 6.0)
    return drawn.astype(jnp.bfloat16)


def query_base(key):
    drawn = jnp.clip(jax.random.normal(jax.random.fold_in(key, 11), (D, HEADS * HEAD_DIM), jnp.float32), -6.0, 6.0)
    return drawn / D ** 0.5


def draw_w_query(key, part):
    return query_base(key).astype(jnp.bfloat16)


def draw_w_key(key, part):
    own_part = jnp.clip(jax.random.normal(jax.random.fold_in(key, 12), (D, KV_HEADS * HEAD_DIM), jnp.float32), -6.0, 6.0) / D ** 0.5
    return own_part.astype(jnp.bfloat16)


def block_scale(key, dims, split, low, high):
    level, own = 1.0, jax.random.fold_in(key, 6)
    for dim, parts in split:
        draws = jnp.exp(jax.random.uniform(jax.random.fold_in(own, dim), (parts,), jnp.float32, low / len(split), high / len(split)))
        level = level * jnp.repeat(draws, dims[dim] // parts).reshape([-1 if axis == dim else 1 for axis in range(len(dims))])
    return level


def centred(own_key, extent, width, most, pieces=(), kind=jnp.bfloat16):
    drawn = jax.random.normal(own_key, extent, jnp.float32) * width
    if len(pieces) > 0:
        drawn = block_scale(own_key, extent, pieces, -0.22, 0.18) * drawn
    return jnp.clip(drawn, min=-most, max=most).astype(kind)


def setup_inputs(seed: int = 0) -> dict:
    streams_of = jax.random.split(jax.random.key(seed), 6)
    tokens = draw_tokens(jax.random.fold_in(streams_of[5], 71), 0)
    w_query = draw_w_query(jax.random.fold_in(streams_of[5], 71), 0)
    w_key = draw_w_key(jax.random.fold_in(streams_of[5], 71), 0)
    w_value = centred(streams_of[3], (D, KV_HEADS * HEAD_DIM), D ** -0.5, 0.09375, ((0, 4), (1, 4)))
    w_output = centred(streams_of[4], (HEADS * HEAD_DIM, D), (HEADS * HEAD_DIM) ** -0.5, 0.09375, ((0, 4), (1, 4)))
    return dict(tokens=tokens, w_query=w_query, w_key=w_key, w_value=w_value, w_output=w_output)


rope_base = 500000.0
masked_score = -1e30


def rotate(values, positions):
    half = HEAD_DIM // 2
    freqs = rope_base ** (-(jnp.arange(half, dtype=jnp.float32) * 2.0) / HEAD_DIM)
    angles = positions.astype(jnp.float32)[:, None] * freqs[None, :]
    cosine = jnp.concatenate([jnp.cos(angles), jnp.cos(angles)], axis=1)
    sine = jnp.concatenate([jnp.sin(angles), jnp.sin(angles)], axis=1)
    count = values.shape[0]
    heads = values.reshape(count, -1, HEAD_DIM)
    turned = jnp.concatenate([-heads[..., half:], heads[..., :half]], axis=-1)
    result = heads * cosine[:, None, :] + turned * sine[:, None, :]
    return result.reshape(count, -1)


def reference(tokens, w_query, w_key, w_value, w_output):
    positions = jnp.arange(SEQ_LEN, dtype=jnp.int32)
    query = rotate(jnp.dot(tokens, w_query, preferred_element_type=jnp.float32), positions).astype(jnp.bfloat16)
    keys = rotate(jnp.dot(tokens, w_key, preferred_element_type=jnp.float32), positions).astype(jnp.bfloat16)
    values = jnp.dot(tokens, w_value, preferred_element_type=jnp.float32).astype(jnp.bfloat16)
    group = HEADS // KV_HEADS
    q_rows = math.gcd(SEQ_LEN, 256)
    key_full = keys.astype(jnp.float32).reshape(SEQ_LEN, KV_HEADS, HEAD_DIM)
    value_full = values.astype(jnp.float32).reshape(SEQ_LEN, KV_HEADS, HEAD_DIM)
    score_scale = HEAD_DIM ** -0.5

    def one_block(index):
        start = index * q_rows
        q_block = lax.dynamic_slice_in_dim(query, start, q_rows, 0).astype(jnp.float32)
        q_block = q_block.reshape(q_rows, KV_HEADS, group, HEAD_DIM)
        scores = jnp.einsum("qgha,kga->ghqk", q_block, key_full) * score_scale
        q_pos = start + jnp.arange(q_rows, dtype=jnp.int32)
        allowed = positions[None, :] <= q_pos[:, None]
        scores = jnp.where(allowed, scores, masked_score)
        peak = jnp.max(scores, axis=-1, keepdims=True)
        weights = jnp.exp(scores - peak)
        total = jnp.sum(weights, axis=-1)
        rounded = lax.optimization_barrier(weights.astype(jnp.bfloat16)).astype(jnp.float32)
        summed = jnp.einsum("ghqk,kga->ghqa", rounded, value_full) / total[..., None]
        return summed.transpose(2, 0, 1, 3).reshape(q_rows, HEADS * HEAD_DIM).astype(jnp.bfloat16)

    heads_out = lax.map(one_block, jnp.arange(SEQ_LEN // q_rows, dtype=jnp.int32))
    heads_out = heads_out.reshape(SEQ_LEN, HEADS * HEAD_DIM)
    return jnp.dot(heads_out, w_output, preferred_element_type=jnp.float32).astype(jnp.bfloat16)
```

```python
import jax
import jax.numpy as jnp
from jax import lax
from jax.sharding import PartitionSpec as P

HEADS = 32
KV_HEADS = 8
HEAD_DIM = 128


rope_base = 500000.0
masked_score = -1e30


def rotate(values, positions):
    half = HEAD_DIM // 2
    freqs = rope_base ** (-(jnp.arange(half, dtype=jnp.float32) * 2.0) / HEAD_DIM)
    angles = positions.astype(jnp.float32)[:, None] * freqs[None, :]
    cosine = jnp.concatenate([jnp.cos(angles), jnp.cos(angles)], axis=1)
    sine = jnp.concatenate([jnp.sin(angles), jnp.sin(angles)], axis=1)
    count = values.shape[0]
    heads = values.reshape(count, -1, HEAD_DIM)
    turned = jnp.concatenate([-heads[..., half:], heads[..., :half]], axis=-1)
    result = heads * cosine[:, None, :] + turned * sine[:, None, :]
    return result.reshape(count, -1)


def swap_pairs(value, flip):
    count = lax.axis_size("row")
    return lax.ppermute(value, "row", [(r, r ^ flip) for r in range(count)])


def pick(flag, first, second):
    return jnp.where(flag, first, second)


def on_device(tokens, w_query, w_key, w_value, w_output):
    shard_rows = tokens.shape[0]
    col_count = lax.axis_size("col")
    row_count = lax.axis_size("row")
    seq_count = lax.axis_size("seq")
    block_len = shard_rows * col_count
    key_len = block_len // 2
    seq_at = lax.axis_index("seq")
    row_at = lax.axis_index("row")
    core = row_at % 2
    chip = row_at // 2
    width_q = w_query.shape[1]
    width_kv = w_key.shape[1]
    local_kv = width_kv // HEAD_DIM
    assert row_count == 2 * local_kv
    q_width = width_q // row_count
    score_scale = HEAD_DIM ** (-0.5)

    block_tokens = lax.all_gather(tokens, "col", axis=0, tiled=True)
    part_q = jnp.dot(block_tokens, w_query, preferred_element_type=jnp.float32)
    part_k = jnp.dot(block_tokens, w_key, preferred_element_type=jnp.float32)
    part_v = jnp.dot(block_tokens, w_value, preferred_element_type=jnp.float32)
    q_chunks = part_q.reshape(block_len, row_count, q_width).transpose(1, 0, 2)
    q_chunks = q_chunks.reshape(2, 2, block_len * q_width // HEAD_DIM, HEAD_DIM)

    def kv_chunks(part):
        split = part.reshape(2, key_len, local_kv, HEAD_DIM).transpose(2, 0, 1, 3)
        return split

    chunks = jnp.concatenate([q_chunks, kv_chunks(part_k), kv_chunks(part_v)], axis=2)
    keep_a = lax.dynamic_index_in_dim(chunks, core, axis=1, keepdims=False)
    send_a = lax.dynamic_index_in_dim(chunks, 1 - core, axis=1, keepdims=False)
    summed_a = keep_a + swap_pairs(send_a, 1)
    keep_b = lax.dynamic_index_in_dim(summed_a, chip, axis=0, keepdims=False)
    send_b = lax.dynamic_index_in_dim(summed_a, 1 - chip, axis=0, keepdims=False)
    mine = keep_b + swap_pairs(send_b.astype(jnp.bfloat16), 2).astype(jnp.float32)

    q_rows = block_len * q_width // HEAD_DIM
    q_mine = mine[:q_rows].reshape(block_len, q_width)
    k_mine = mine[q_rows : q_rows + key_len]
    v_mine = mine[q_rows + key_len :]

    block_start = seq_at * block_len
    q_pos = block_start + jnp.arange(block_len, dtype=jnp.int32)
    k_offset = core * key_len + jnp.arange(key_len, dtype=jnp.int32)
    query = rotate(q_mine, q_pos).astype(jnp.bfloat16)
    keys = rotate(k_mine, block_start + k_offset).astype(jnp.bfloat16)
    kv_own = jnp.concatenate([keys, v_mine.astype(jnp.bfloat16)], axis=1)

    query_other = swap_pairs(query, 1)
    q_all = jnp.concatenate([query, query_other], axis=1)
    q_heads = q_all.reshape(block_len, -1, HEAD_DIM).transpose(1, 0, 2)
    n_heads = q_heads.shape[0]

    def attend(state, kv_rows, key_pos):
        peak, total, summed = state
        key_blk = kv_rows[:, :HEAD_DIM]
        value_blk = kv_rows[:, HEAD_DIM:]
        scores = (
            jnp.einsum("hqd,kd->hqk", q_heads, key_blk, preferred_element_type=jnp.float32)
            * score_scale
        )
        allowed = key_pos[None, :] <= q_pos[:, None]
        scores = jnp.where(allowed[None], scores, masked_score)
        new_peak = jnp.maximum(peak, jnp.max(scores, axis=-1))
        weights = jnp.exp(scores - new_peak[..., None])
        factor = jnp.exp(peak - new_peak)
        total = total * factor + jnp.sum(weights, axis=-1)
        summed = summed * factor[..., None] + jnp.einsum(
            "hqk,kd->hqd",
            weights.astype(jnp.bfloat16),
            value_blk,
            preferred_element_type=jnp.float32,
        )
        return (new_peak, total, summed)

    state = (
        jnp.full((n_heads, block_len), masked_score, jnp.float32),
        jnp.zeros((n_heads, block_len), jnp.float32),
        jnp.zeros((n_heads, block_len, HEAD_DIM), jnp.float32),
    )
    ring = [(s, (s + 1) % seq_count) for s in range(seq_count)]
    kv_here = kv_own
    for step in range(seq_count):
        if step > 0:
            kv_here = lax.ppermute(kv_here, "seq", ring)
        source = (seq_at - step) % seq_count
        state = attend(state, kv_here, source * block_len + k_offset)

    peak, total, summed = state
    own = n_heads // 2
    other_peak, other_total, other_summed = swap_pairs(
        (peak[own:], total[own:], summed[own:]), 1
    )
    peak_mine = jnp.maximum(peak[:own], other_peak)
    factor_a = jnp.exp(peak[:own] - peak_mine)
    factor_b = jnp.exp(other_peak - peak_mine)
    total_mine = total[:own] * factor_a + other_total * factor_b
    summed_mine = summed[:own] * factor_a[..., None] + other_summed * factor_b[..., None]
    heads_mine = (summed_mine / total_mine[..., None]).transpose(1, 0, 2)
    heads_mine = heads_mine.reshape(block_len, q_width).astype(jnp.bfloat16)

    heads_pair_other = swap_pairs(heads_mine, 1)
    heads_pair = jnp.stack(
        [pick(core == 0, heads_mine, heads_pair_other), pick(core == 0, heads_pair_other, heads_mine)]
    )
    heads_quad_other = swap_pairs(heads_pair, 2)
    heads_quad = jnp.concatenate(
        [pick(chip == 0, heads_pair, heads_quad_other), pick(chip == 0, heads_quad_other, heads_pair)]
    )
    w_out = w_output.reshape(row_count, q_width, w_output.shape[1])
    partial_out = jnp.einsum(
        "rtc,rco->to", heads_quad, w_out, preferred_element_type=jnp.float32
    ).astype(jnp.bfloat16)
    return lax.psum_scatter(partial_out, "col", scatter_dimension=0, tiled=True)


def solution(mesh):
    return jax.shard_map(
        on_device,
        mesh=mesh,
        in_specs=(
            P(("seq", "col"), "row"),
            P("row", "col"),
            P("row", "col"),
            P("row", "col"),
            P("col", "row"),
        ),
        out_specs=P(("seq", "col"), "row"),
        check_vma=False,
    )
```

```python
import jax
import jax.numpy as jnp
from jax import lax
from jax.sharding import PartitionSpec as P

HEADS = 32
KV_HEADS = 8
HEAD_DIM = 128


rope_base = 500000.0
masked_score = -1e30


def rotate(values, positions):
    half = HEAD_DIM // 2
    freqs = rope_base ** (-(jnp.arange(half, dtype=jnp.float32) * 2.0) / HEAD_DIM)
    angles = positions.astype(jnp.float32)[:, None] * freqs[None, :]
    cosine = jnp.concatenate([jnp.cos(angles), jnp.cos(angles)], axis=1)
    sine = jnp.concatenate([jnp.sin(angles), jnp.sin(angles)], axis=1)
    count = values.shape[0]
    heads = values.reshape(count, -1, HEAD_DIM)
    turned = jnp.concatenate([-heads[..., half:], heads[..., :half]], axis=-1)
    result = heads * cosine[:, None, :] + turned * sine[:, None, :]
    return result.reshape(count, -1)


def swap_pairs(value, flip):
    count = lax.axis_size("row")
    return lax.ppermute(value, "row", [(r, r ^ flip) for r in range(count)])


def shifted(value, axis, step):
    count = lax.axis_size(axis)
    return lax.ppermute(value, axis, [(i, (i + step) % count) for i in range(count)])


def pick(flag, first, second):
    return jnp.where(flag, first, second)


def on_device(tokens, w_query, w_key, w_value, w_output):
    shard_rows = tokens.shape[0]
    col_count = lax.axis_size("col")
    row_count = lax.axis_size("row")
    seq_count = lax.axis_size("seq")
    block_len = shard_rows * col_count
    key_len = block_len // 2
    seq_at = lax.axis_index("seq")
    row_at = lax.axis_index("row")
    core = row_at % 2
    chip = row_at // 2
    width_q = w_query.shape[1]
    width_kv = w_key.shape[1]
    local_kv = width_kv // HEAD_DIM
    assert row_count == 2 * local_kv
    q_width = width_q // row_count
    score_scale = HEAD_DIM ** (-0.5)

    col_at = lax.axis_index("col")
    pieces = [tokens] + [shifted(tokens, "col", step) for step in range(1, col_count)]
    order = (col_at - jnp.arange(col_count, dtype=jnp.int32)) % col_count
    block_tokens = jnp.take(jnp.stack(pieces), order, axis=0).reshape(block_len, -1)
    part_q = jnp.dot(block_tokens, w_query, preferred_element_type=jnp.float32)
    part_k = jnp.dot(block_tokens, w_key, preferred_element_type=jnp.float32)
    part_v = jnp.dot(block_tokens, w_value, preferred_element_type=jnp.float32)
    q_chunks = part_q.reshape(block_len, row_count, q_width).transpose(1, 0, 2)
    q_chunks = q_chunks.reshape(2, 2, block_len * q_width // HEAD_DIM, HEAD_DIM)

    def kv_chunks(part):
        split = part.reshape(2, key_len, local_kv, HEAD_DIM).transpose(2, 0, 1, 3)
        return split

    chunks = jnp.concatenate([q_chunks, kv_chunks(part_k), kv_chunks(part_v)], axis=2)
    keep_a = lax.dynamic_index_in_dim(chunks, core, axis=1, keepdims=False)
    send_a = lax.dynamic_index_in_dim(chunks, 1 - core, axis=1, keepdims=False)
    summed_a = keep_a + swap_pairs(send_a, 1)
    keep_b = lax.dynamic_index_in_dim(summed_a, chip, axis=0, keepdims=False)
    send_b = lax.dynamic_index_in_dim(summed_a, 1 - chip, axis=0, keepdims=False)
    mine = keep_b + swap_pairs(send_b.astype(jnp.bfloat16), 2).astype(jnp.float32)

    q_rows = block_len * q_width // HEAD_DIM
    q_mine = mine[:q_rows].reshape(block_len, q_width)
    k_mine = mine[q_rows : q_rows + key_len]
    v_mine = mine[q_rows + key_len :]

    block_start = seq_at * block_len
    q_pos = block_start + jnp.arange(block_len, dtype=jnp.int32)
    k_offset = core * key_len + jnp.arange(key_len, dtype=jnp.int32)
    query = rotate(q_mine, q_pos).astype(jnp.bfloat16)
    keys = rotate(k_mine, block_start + k_offset).astype(jnp.bfloat16)
    kv_own = jnp.concatenate([keys, v_mine.astype(jnp.bfloat16)], axis=1)

    query_other = swap_pairs(query, 1)
    q_all = jnp.concatenate([query, query_other], axis=1)
    q_heads = q_all.reshape(block_len, -1, HEAD_DIM).transpose(1, 0, 2)
    n_heads = q_heads.shape[0]

    def attend(state, kv_rows, allowed):
        peak, total, summed = state
        key_blk = kv_rows[:, :HEAD_DIM]
        value_blk = kv_rows[:, HEAD_DIM:]
        scores = (
            jnp.einsum("hqd,kd->hqk", q_heads, key_blk, preferred_element_type=jnp.float32)
            * score_scale
        )
        scores = jnp.where(allowed[None], scores, masked_score)
        new_peak = jnp.maximum(peak, jnp.max(scores, axis=-1))
        weights = jnp.exp(scores - new_peak[..., None])
        factor = jnp.exp(peak - new_peak)
        total = total * factor + jnp.sum(weights, axis=-1)
        summed = summed * factor[..., None] + jnp.einsum(
            "hqk,kd->hqd",
            weights.astype(jnp.bfloat16),
            value_blk,
            preferred_element_type=jnp.float32,
        )
        return (new_peak, total, summed)

    state = (
        jnp.full((n_heads, block_len), masked_score, jnp.float32),
        jnp.zeros((n_heads, block_len), jnp.float32),
        jnp.zeros((n_heads, block_len, HEAD_DIM), jnp.float32),
    )
    kv_all = lax.all_gather(kv_own, "seq", axis=0, tiled=False)
    own_pos = block_start + k_offset
    state = attend(state, kv_own, own_pos[None, :] <= q_pos[:, None])
    per_chunk = 4
    for first in range(0, seq_count, per_chunk):
        kv_chunk = kv_all[first : first + per_chunk].reshape(per_chunk * key_len, -1)
        blocks = first + jnp.arange(per_chunk, dtype=jnp.int32)
        chunk_pos = (blocks[:, None] * block_len + k_offset[None, :]).reshape(-1)
        state = attend(state, kv_chunk, (chunk_pos < block_start)[None, :])

    peak, total, summed = state
    own = n_heads // 2
    other_peak, other_total, other_summed = swap_pairs(
        (peak[own:], total[own:], summed[own:]), 1
    )
    peak_mine = jnp.maximum(peak[:own], other_peak)
    factor_a = jnp.exp(peak[:own] - peak_mine)
    factor_b = jnp.exp(other_peak - peak_mine)
    total_mine = total[:own] * factor_a + other_total * factor_b
    summed_mine = summed[:own] * factor_a[..., None] + other_summed * factor_b[..., None]
    heads_mine = (summed_mine / total_mine[..., None]).transpose(1, 0, 2)
    heads_mine = heads_mine.reshape(block_len, q_width).astype(jnp.bfloat16)

    heads_pair_other = swap_pairs(heads_mine, 1)
    heads_pair = jnp.stack(
        [pick(core == 0, heads_mine, heads_pair_other), pick(core == 0, heads_pair_other, heads_mine)]
    )
    heads_quad_other = swap_pairs(heads_pair, 2)
    heads_quad = jnp.concatenate(
        [pick(chip == 0, heads_pair, heads_quad_other), pick(chip == 0, heads_quad_other, heads_pair)]
    )
    w_out = w_output.reshape(row_count, q_width, w_output.shape[1])
    partial_out = jnp.einsum(
        "rtc,rco->to", heads_quad, w_out, preferred_element_type=jnp.float32
    ).astype(jnp.bfloat16)
    out_chunks = partial_out.reshape(col_count, shard_rows, -1)
    result = lax.dynamic_index_in_dim(out_chunks, col_at, 0, keepdims=False).astype(jnp.float32)
    for step in range(1, col_count):
        target = (col_at + step) % col_count
        sent = lax.dynamic_index_in_dim(out_chunks, target, 0, keepdims=False)
        result = result + shifted(sent, "col", step).astype(jnp.float32)
    return result.astype(jnp.bfloat16)


def solution(mesh):
    return jax.shard_map(
        on_device,
        mesh=mesh,
        in_specs=(
            P(("seq", "col"), "row"),
            P("row", "col"),
            P("row", "col"),
            P("row", "col"),
            P("col", "row"),
        ),
        out_specs=P(("seq", "col"), "row"),
        check_vma=False,
    )
```

```python
import jax
import jax.numpy as jnp
from jax import lax
from jax.sharding import PartitionSpec as P

HEADS = 32
KV_HEADS = 8
HEAD_DIM = 128


rope_base = 500000.0
masked_score = -1e30


def rotate(values, positions):
    half = HEAD_DIM // 2
    freqs = rope_base ** (-(jnp.arange(half, dtype=jnp.float32) * 2.0) / HEAD_DIM)
    angles = positions.astype(jnp.float32)[:, None] * freqs[None, :]
    cosine = jnp.concatenate([jnp.cos(angles), jnp.cos(angles)], axis=1)
    sine = jnp.concatenate([jnp.sin(angles), jnp.sin(angles)], axis=1)
    count = values.shape[0]
    heads = values.reshape(count, -1, HEAD_DIM)
    turned = jnp.concatenate([-heads[..., half:], heads[..., :half]], axis=-1)
    result = heads * cosine[:, None, :] + turned * sine[:, None, :]
    return result.reshape(count, -1)


def swap_pairs(value, flip):
    count = lax.axis_size("row")
    return lax.ppermute(value, "row", [(r, r ^ flip) for r in range(count)])


def shifted(value, axis, step):
    count = lax.axis_size(axis)
    return lax.ppermute(value, axis, [(i, (i + step) % count) for i in range(count)])


def pick(flag, first, second):
    return jnp.where(flag, first, second)


def on_device(tokens, w_query, w_key, w_value, w_output):
    shard_rows = tokens.shape[0]
    col_count = lax.axis_size("col")
    row_count = lax.axis_size("row")
    seq_count = lax.axis_size("seq")
    block_len = shard_rows * col_count
    key_len = block_len // 2
    seq_at = lax.axis_index("seq")
    row_at = lax.axis_index("row")
    core = row_at % 2
    chip = row_at // 2
    width_q = w_query.shape[1]
    width_kv = w_key.shape[1]
    local_kv = width_kv // HEAD_DIM
    assert row_count == 2 * local_kv
    q_width = width_q // row_count
    score_scale = HEAD_DIM ** (-0.5)

    col_at = lax.axis_index("col")
    pieces = [tokens] + [shifted(tokens, "col", step) for step in range(1, col_count)]
    order = (col_at - jnp.arange(col_count, dtype=jnp.int32)) % col_count
    block_tokens = jnp.take(jnp.stack(pieces), order, axis=0).reshape(block_len, -1)
    part_q = jnp.dot(block_tokens, w_query, preferred_element_type=jnp.float32)
    part_k = jnp.dot(block_tokens, w_key, preferred_element_type=jnp.float32)
    part_v = jnp.dot(block_tokens, w_value, preferred_element_type=jnp.float32)
    q_chunks = part_q.reshape(block_len, row_count, q_width).transpose(1, 0, 2)
    q_chunks = q_chunks.reshape(2, 2, block_len * q_width // HEAD_DIM, HEAD_DIM)

    def kv_chunks(part):
        split = part.reshape(2, key_len, local_kv, HEAD_DIM).transpose(2, 0, 1, 3)
        return split

    chunks = jnp.concatenate([q_chunks, kv_chunks(part_k), kv_chunks(part_v)], axis=2)
    keep_a = lax.dynamic_index_in_dim(chunks, core, axis=1, keepdims=False)
    send_a = lax.dynamic_index_in_dim(chunks, 1 - core, axis=1, keepdims=False)
    summed_a = keep_a + swap_pairs(send_a, 1)
    keep_b = lax.dynamic_index_in_dim(summed_a, chip, axis=0, keepdims=False)
    send_b = lax.dynamic_index_in_dim(summed_a, 1 - chip, axis=0, keepdims=False)
    mine = keep_b + swap_pairs(send_b.astype(jnp.bfloat16), 2).astype(jnp.float32)

    q_rows = block_len * q_width // HEAD_DIM
    q_mine = mine[:q_rows].reshape(block_len, q_width)
    k_mine = mine[q_rows : q_rows + key_len]
    v_mine = mine[q_rows + key_len :]

    block_start = seq_at * block_len
    q_pos = block_start + jnp.arange(block_len, dtype=jnp.int32)
    k_offset = core * key_len + jnp.arange(key_len, dtype=jnp.int32)
    query = rotate(q_mine, q_pos).astype(jnp.bfloat16)
    keys = rotate(k_mine, block_start + k_offset).astype(jnp.bfloat16)
    kv_own = jnp.concatenate([keys, v_mine.astype(jnp.bfloat16)], axis=1)

    query_other = swap_pairs(query, 1)
    q_all = jnp.concatenate([query, query_other], axis=1)
    q_heads = q_all.reshape(block_len, -1, HEAD_DIM).transpose(1, 0, 2)
    n_heads = q_heads.shape[0]

    def attend(state, kv_rows, allowed):
        peak, total, summed = state
        key_blk = kv_rows[:, :HEAD_DIM]
        value_blk = kv_rows[:, HEAD_DIM:]
        scores = (
            jnp.einsum("hqd,kd->hqk", q_heads, key_blk, preferred_element_type=jnp.float32)
            * score_scale
        )
        scores = jnp.where(allowed[None], scores, masked_score)
        new_peak = jnp.maximum(peak, jnp.max(scores, axis=-1))
        weights = jnp.exp(scores - new_peak[..., None])
        factor = jnp.exp(peak - new_peak)
        total = total * factor + jnp.sum(weights, axis=-1)
        summed = summed * factor[..., None] + jnp.einsum(
            "hqk,kd->hqd",
            weights.astype(jnp.bfloat16),
            value_blk,
            preferred_element_type=jnp.float32,
        )
        return (new_peak, total, summed)

    state = (
        jnp.full((n_heads, block_len), masked_score, jnp.float32),
        jnp.zeros((n_heads, block_len), jnp.float32),
        jnp.zeros((n_heads, block_len, HEAD_DIM), jnp.float32),
    )
    parts = 1
    part_len = key_len // parts
    kv_parts = kv_own.reshape(parts, part_len, -1)
    gathered = [
        lax.all_gather(kv_parts[p].reshape(-1), "seq", axis=0, tiled=True).reshape(seq_count, part_len, -1)
        for p in range(parts)
    ]
    own_pos = block_start + k_offset
    state = attend(state, kv_own, own_pos[None, :] <= q_pos[:, None])
    per_chunk = seq_count // 2
    for p in range(parts):
        for first in range(0, seq_count, per_chunk):
            kv_chunk = gathered[p][first : first + per_chunk].reshape(per_chunk * part_len, -1)
            blocks = first + jnp.arange(per_chunk, dtype=jnp.int32)
            part_offset = core * key_len + p * part_len + jnp.arange(part_len, dtype=jnp.int32)
            chunk_pos = (blocks[:, None] * block_len + part_offset[None, :]).reshape(-1)
            state = attend(state, kv_chunk, (chunk_pos < block_start)[None, :])

    peak, total, summed = state
    own = n_heads // 2
    other_peak, other_total, other_summed = swap_pairs(
        (peak[own:], total[own:], summed[own:]), 1
    )
    peak_mine = jnp.maximum(peak[:own], other_peak)
    factor_a = jnp.exp(peak[:own] - peak_mine)
    factor_b = jnp.exp(other_peak - peak_mine)
    total_mine = total[:own] * factor_a + other_total * factor_b
    summed_mine = summed[:own] * factor_a[..., None] + other_summed * factor_b[..., None]
    heads_mine = (summed_mine / total_mine[..., None]).transpose(1, 0, 2)
    heads_mine = heads_mine.reshape(block_len, q_width).astype(jnp.bfloat16)

    heads_pair_other = swap_pairs(heads_mine, 1)
    heads_pair = jnp.stack(
        [pick(core == 0, heads_mine, heads_pair_other), pick(core == 0, heads_pair_other, heads_mine)]
    )
    heads_quad_other = swap_pairs(heads_pair, 2)
    heads_quad = jnp.concatenate(
        [pick(chip == 0, heads_pair, heads_quad_other), pick(chip == 0, heads_quad_other, heads_pair)]
    )
    w_out = w_output.reshape(row_count, q_width, w_output.shape[1])
    partial_out = jnp.einsum(
        "rtc,rco->to", heads_quad, w_out, preferred_element_type=jnp.float32
    ).astype(jnp.bfloat16)
    out_chunks = partial_out.reshape(col_count, shard_rows, -1)
    result = lax.dynamic_index_in_dim(out_chunks, col_at, 0, keepdims=False).astype(jnp.float32)
    for step in range(1, col_count):
        target = (col_at + step) % col_count
        sent = lax.dynamic_index_in_dim(out_chunks, target, 0, keepdims=False)
        result = result + shifted(sent, "col", step).astype(jnp.float32)
    return result.astype(jnp.bfloat16)


def solution(mesh):
    return jax.shard_map(
        on_device,
        mesh=mesh,
        in_specs=(
            P(("seq", "col"), "row"),
            P("row", "col"),
            P("row", "col"),
            P("row", "col"),
            P("col", "row"),
        ),
        out_specs=P(("seq", "col"), "row"),
        check_vma=False,
    )
```

```python
import jax
import jax.numpy as jnp
from jax import lax
from jax.sharding import PartitionSpec as P

HEADS = 32
KV_HEADS = 8
HEAD_DIM = 128


rope_base = 500000.0
masked_score = -1e30


def rotate(values, positions):
    half = HEAD_DIM // 2
    freqs = rope_base ** (-(jnp.arange(half, dtype=jnp.float32) * 2.0) / HEAD_DIM)
    angles = positions.astype(jnp.float32)[:, None] * freqs[None, :]
    cosine = jnp.concatenate([jnp.cos(angles), jnp.cos(angles)], axis=1)
    sine = jnp.concatenate([jnp.sin(angles), jnp.sin(angles)], axis=1)
    count = values.shape[0]
    heads = values.reshape(count, -1, HEAD_DIM)
    turned = jnp.concatenate([-heads[..., half:], heads[..., :half]], axis=-1)
    result = heads * cosine[:, None, :] + turned * sine[:, None, :]
    return result.reshape(count, -1)


def swap_pairs(value, flip):
    count = lax.axis_size("row")
    return lax.ppermute(value, "row", [(r, r ^ flip) for r in range(count)])


def shifted(value, axis, step):
    count = lax.axis_size(axis)
    return lax.ppermute(value, axis, [(i, (i + step) % count) for i in range(count)])


def pick(flag, first, second):
    return jnp.where(flag, first, second)


def on_device(tokens, w_query, w_key, w_value, w_output):
    shard_rows = tokens.shape[0]
    col_count = lax.axis_size("col")
    row_count = lax.axis_size("row")
    seq_count = lax.axis_size("seq")
    block_len = shard_rows * col_count
    key_len = block_len // 2
    seq_at = lax.axis_index("seq")
    row_at = lax.axis_index("row")
    core = row_at % 2
    chip = row_at // 2
    width_q = w_query.shape[1]
    width_kv = w_key.shape[1]
    local_kv = width_kv // HEAD_DIM
    assert row_count == 2 * local_kv
    q_width = width_q // row_count
    score_scale = HEAD_DIM ** (-0.5)

    col_at = lax.axis_index("col")
    pieces = [tokens] + [shifted(tokens, "col", step) for step in range(1, col_count)]
    order = (col_at - jnp.arange(col_count, dtype=jnp.int32)) % col_count
    block_tokens = jnp.take(jnp.stack(pieces), order, axis=0).reshape(block_len, -1)
    part_q = jnp.dot(block_tokens, w_query, preferred_element_type=jnp.float32)
    part_k = jnp.dot(block_tokens, w_key, preferred_element_type=jnp.float32)
    part_v = jnp.dot(block_tokens, w_value, preferred_element_type=jnp.float32)
    q_chunks = part_q.reshape(block_len, row_count, q_width).transpose(1, 0, 2)
    q_chunks = q_chunks.reshape(2, 2, block_len * q_width // HEAD_DIM, HEAD_DIM)

    def kv_chunks(part):
        split = part.reshape(2, key_len, local_kv, HEAD_DIM).transpose(2, 0, 1, 3)
        return split

    chunks = jnp.concatenate([q_chunks, kv_chunks(part_k), kv_chunks(part_v)], axis=2)
    keep_a = lax.dynamic_index_in_dim(chunks, core, axis=1, keepdims=False)
    send_a = lax.dynamic_index_in_dim(chunks, 1 - core, axis=1, keepdims=False)
    summed_a = keep_a + swap_pairs(send_a, 1)
    keep_b = lax.dynamic_index_in_dim(summed_a, chip, axis=0, keepdims=False)
    send_b = lax.dynamic_index_in_dim(summed_a, 1 - chip, axis=0, keepdims=False)
    mine = keep_b + swap_pairs(send_b.astype(jnp.bfloat16), 2).astype(jnp.float32)

    q_rows = block_len * q_width // HEAD_DIM
    q_mine = mine[:q_rows].reshape(block_len, q_width)
    k_mine = mine[q_rows : q_rows + key_len]
    v_mine = mine[q_rows + key_len :]

    block_start = seq_at * block_len
    q_pos = block_start + jnp.arange(block_len, dtype=jnp.int32)
    k_offset = core * key_len + jnp.arange(key_len, dtype=jnp.int32)
    query = rotate(q_mine, q_pos).astype(jnp.bfloat16)
    keys = rotate(k_mine, block_start + k_offset).astype(jnp.bfloat16)
    kv_own = jnp.concatenate([keys, v_mine.astype(jnp.bfloat16)], axis=1)

    query_other = swap_pairs(query, 1)
    q_all = jnp.concatenate([query, query_other], axis=1)
    q_heads = q_all.reshape(block_len, -1, HEAD_DIM).transpose(1, 0, 2)
    n_heads = q_heads.shape[0]

    def attend(state, kv_rows, allowed):
        peak, total, summed = state
        key_blk = kv_rows[:, :HEAD_DIM]
        value_blk = kv_rows[:, HEAD_DIM:]
        scores = (
            jnp.einsum("hqd,kd->hqk", q_heads, key_blk, preferred_element_type=jnp.float32)
            * score_scale
        )
        scores = jnp.where(allowed[None], scores, masked_score)
        new_peak = jnp.maximum(peak, jnp.max(scores, axis=-1))
        weights = jnp.exp(scores - new_peak[..., None])
        factor = jnp.exp(peak - new_peak)
        total = total * factor + jnp.sum(weights, axis=-1)
        summed = summed * factor[..., None] + jnp.einsum(
            "hqk,kd->hqd",
            weights.astype(jnp.bfloat16),
            value_blk,
            preferred_element_type=jnp.float32,
        )
        return (new_peak, total, summed)

    state = (
        jnp.full((n_heads, block_len), masked_score, jnp.float32),
        jnp.zeros((n_heads, block_len), jnp.float32),
        jnp.zeros((n_heads, block_len, HEAD_DIM), jnp.float32),
    )
    own_pos = block_start + k_offset
    state = attend(state, kv_own, own_pos[None, :] <= q_pos[:, None])
    forward = [(s, (s + 1) % seq_count) for s in range(seq_count)]
    backward = [(s, (s - 1) % seq_count) for s in range(seq_count)]
    kv_fwd = kv_own
    kv_bwd = kv_own
    for step in range(1, seq_count // 2 + 1):
        kv_fwd = lax.ppermute(kv_fwd, "seq", forward)
        if step < seq_count // 2:
            kv_bwd = lax.ppermute(kv_bwd, "seq", backward)
        fwd_pos = ((seq_at - step) % seq_count) * block_len + k_offset
        state = attend(state, kv_fwd, (fwd_pos < block_start)[None, :])
        if step < seq_count // 2:
            bwd_pos = ((seq_at + step) % seq_count) * block_len + k_offset
            state = attend(state, kv_bwd, (bwd_pos < block_start)[None, :])

    peak, total, summed = state
    own = n_heads // 2
    other_peak, other_total, other_summed = swap_pairs(
        (peak[own:], total[own:], summed[own:]), 1
    )
    peak_mine = jnp.maximum(peak[:own], other_peak)
    factor_a = jnp.exp(peak[:own] - peak_mine)
    factor_b = jnp.exp(other_peak - peak_mine)
    total_mine = total[:own] * factor_a + other_total * factor_b
    summed_mine = summed[:own] * factor_a[..., None] + other_summed * factor_b[..., None]
    heads_mine = (summed_mine / total_mine[..., None]).transpose(1, 0, 2)
    heads_mine = heads_mine.reshape(block_len, q_width).astype(jnp.bfloat16)

    heads_pair_other = swap_pairs(heads_mine, 1)
    heads_pair = jnp.stack(
        [pick(core == 0, heads_mine, heads_pair_other), pick(core == 0, heads_pair_other, heads_mine)]
    )
    heads_quad_other = swap_pairs(heads_pair, 2)
    heads_quad = jnp.concatenate(
        [pick(chip == 0, heads_pair, heads_quad_other), pick(chip == 0, heads_quad_other, heads_pair)]
    )
    w_out = w_output.reshape(row_count, q_width, w_output.shape[1])
    partial_out = jnp.einsum(
        "rtc,rco->to", heads_quad, w_out, preferred_element_type=jnp.float32
    ).astype(jnp.bfloat16)
    out_chunks = partial_out.reshape(col_count, shard_rows, -1)
    result = lax.dynamic_index_in_dim(out_chunks, col_at, 0, keepdims=False).astype(jnp.float32)
    for step in range(1, col_count):
        target = (col_at + step) % col_count
        sent = lax.dynamic_index_in_dim(out_chunks, target, 0, keepdims=False)
        result = result + shifted(sent, "col", step).astype(jnp.float32)
    return result.astype(jnp.bfloat16)


def solution(mesh):
    return jax.shard_map(
        on_device,
        mesh=mesh,
        in_specs=(
            P(("seq", "col"), "row"),
            P("row", "col"),
            P("row", "col"),
            P("row", "col"),
            P("col", "row"),
        ),
        out_specs=P(("seq", "col"), "row"),
        check_vma=False,
    )
```

```python
import jax
import jax.numpy as jnp
from jax import lax
from jax.sharding import PartitionSpec as P

HEADS = 32
KV_HEADS = 8
HEAD_DIM = 128


rope_base = 500000.0
masked_score = -1e30


def rotate(values, positions):
    half = HEAD_DIM // 2
    freqs = rope_base ** (-(jnp.arange(half, dtype=jnp.float32) * 2.0) / HEAD_DIM)
    angles = positions.astype(jnp.float32)[:, None] * freqs[None, :]
    cosine = jnp.concatenate([jnp.cos(angles), jnp.cos(angles)], axis=1)
    sine = jnp.concatenate([jnp.sin(angles), jnp.sin(angles)], axis=1)
    count = values.shape[0]
    heads = values.reshape(count, -1, HEAD_DIM)
    turned = jnp.concatenate([-heads[..., half:], heads[..., :half]], axis=-1)
    result = heads * cosine[:, None, :] + turned * sine[:, None, :]
    return result.reshape(count, -1)


def swap_pairs(value, flip):
    count = lax.axis_size("row")
    return lax.ppermute(value, "row", [(r, r ^ flip) for r in range(count)])


def shifted(value, axis, step):
    count = lax.axis_size(axis)
    return lax.ppermute(value, axis, [(i, (i + step) % count) for i in range(count)])


def pick(flag, first, second):
    return jnp.where(flag, first, second)


def on_device(tokens, w_query, w_key, w_value, w_output):
    shard_rows = tokens.shape[0]
    col_count = lax.axis_size("col")
    row_count = lax.axis_size("row")
    seq_count = lax.axis_size("seq")
    block_len = shard_rows * col_count
    key_len = block_len // 2
    seq_at = lax.axis_index("seq")
    row_at = lax.axis_index("row")
    core = row_at % 2
    chip = row_at // 2
    width_q = w_query.shape[1]
    width_kv = w_key.shape[1]
    local_kv = width_kv // HEAD_DIM
    assert row_count == 2 * local_kv
    q_width = width_q // row_count
    score_scale = HEAD_DIM ** (-0.5)

    col_at = lax.axis_index("col")
    pieces = [tokens] + [shifted(tokens, "col", step) for step in range(1, col_count)]
    order = (col_at - jnp.arange(col_count, dtype=jnp.int32)) % col_count
    block_tokens = jnp.take(jnp.stack(pieces), order, axis=0).reshape(block_len, -1)
    part_q = jnp.dot(block_tokens, w_query, preferred_element_type=jnp.float32)
    part_k = jnp.dot(block_tokens, w_key, preferred_element_type=jnp.float32)
    part_v = jnp.dot(block_tokens, w_value, preferred_element_type=jnp.float32)
    q_chunks = part_q.reshape(block_len, row_count, q_width).transpose(1, 0, 2)
    q_chunks = q_chunks.reshape(2, 2, block_len * q_width // HEAD_DIM, HEAD_DIM)

    def kv_chunks(part):
        split = part.reshape(2, key_len, local_kv, HEAD_DIM).transpose(2, 0, 1, 3)
        return split

    chunks = jnp.concatenate([q_chunks, kv_chunks(part_k), kv_chunks(part_v)], axis=2)
    keep_a = lax.dynamic_index_in_dim(chunks, core, axis=1, keepdims=False)
    send_a = lax.dynamic_index_in_dim(chunks, 1 - core, axis=1, keepdims=False)
    summed_a = keep_a + swap_pairs(send_a.astype(jnp.bfloat16), 1).astype(jnp.float32)
    keep_b = lax.dynamic_index_in_dim(summed_a, chip, axis=0, keepdims=False)
    send_b = lax.dynamic_index_in_dim(summed_a, 1 - chip, axis=0, keepdims=False)
    mine = keep_b + swap_pairs(send_b.astype(jnp.bfloat16), 2).astype(jnp.float32)

    q_rows = block_len * q_width // HEAD_DIM
    q_mine = mine[:q_rows].reshape(block_len, q_width)
    k_mine = mine[q_rows : q_rows + key_len]
    v_mine = mine[q_rows + key_len :]

    block_start = seq_at * block_len
    q_pos = block_start + jnp.arange(block_len, dtype=jnp.int32)
    k_offset = core * key_len + jnp.arange(key_len, dtype=jnp.int32)
    query = rotate(q_mine, q_pos).astype(jnp.bfloat16)
    keys = rotate(k_mine, block_start + k_offset).astype(jnp.bfloat16)
    kv_own = jnp.concatenate([keys, v_mine.astype(jnp.bfloat16)], axis=1)

    query_other = swap_pairs(query, 1)
    q_all = jnp.concatenate([query, query_other], axis=1)
    q_heads = q_all.reshape(block_len, -1, HEAD_DIM).transpose(1, 0, 2)
    n_heads = q_heads.shape[0]

    def attend(state, kv_rows, allowed):
        peak, total, summed = state
        key_blk = kv_rows[:, :HEAD_DIM]
        value_blk = kv_rows[:, HEAD_DIM:]
        scores = (
            jnp.einsum("hqd,kd->hqk", q_heads, key_blk, preferred_element_type=jnp.float32)
            * score_scale
        )
        scores = jnp.where(allowed[None], scores, masked_score)
        new_peak = jnp.maximum(peak, jnp.max(scores, axis=-1))
        weights = jnp.exp(scores - new_peak[..., None])
        factor = jnp.exp(peak - new_peak)
        total = total * factor + jnp.sum(weights, axis=-1)
        summed = summed * factor[..., None] + jnp.einsum(
            "hqk,kd->hqd",
            weights.astype(jnp.bfloat16),
            value_blk,
            preferred_element_type=jnp.float32,
        )
        return (new_peak, total, summed)

    state = (
        jnp.full((n_heads, block_len), masked_score, jnp.float32),
        jnp.zeros((n_heads, block_len), jnp.float32),
        jnp.zeros((n_heads, block_len, HEAD_DIM), jnp.float32),
    )
    own_pos = block_start + k_offset
    state = attend(state, kv_own, own_pos[None, :] <= q_pos[:, None])
    forward = [(s, (s + 1) % seq_count) for s in range(seq_count)]
    backward = [(s, (s - 1) % seq_count) for s in range(seq_count)]
    kv_fwd = kv_own
    kv_bwd = kv_own
    for step in range(1, seq_count // 2 + 1):
        kv_fwd = lax.ppermute(kv_fwd, "seq", forward)
        if step < seq_count // 2:
            kv_bwd = lax.ppermute(kv_bwd, "seq", backward)
        kv_fwd, kv_bwd, state = lax.optimization_barrier((kv_fwd, kv_bwd, state))
        fwd_pos = ((seq_at - step) % seq_count) * block_len + k_offset
        state = attend(state, kv_fwd, (fwd_pos < block_start)[None, :])
        if step < seq_count // 2:
            bwd_pos = ((seq_at + step) % seq_count) * block_len + k_offset
            state = attend(state, kv_bwd, (bwd_pos < block_start)[None, :])

    peak, total, summed = state
    own = n_heads // 2
    other_peak, other_total, other_summed = swap_pairs(
        (peak[own:], total[own:], summed[own:]), 1
    )
    peak_mine = jnp.maximum(peak[:own], other_peak)
    factor_a = jnp.exp(peak[:own] - peak_mine)
    factor_b = jnp.exp(other_peak - peak_mine)
    total_mine = total[:own] * factor_a + other_total * factor_b
    summed_mine = summed[:own] * factor_a[..., None] + other_summed * factor_b[..., None]
    heads_mine = (summed_mine / total_mine[..., None]).transpose(1, 0, 2)
    heads_mine = heads_mine.reshape(block_len, q_width).astype(jnp.bfloat16)

    heads_pair_other = swap_pairs(heads_mine, 1)
    heads_pair = jnp.stack(
        [pick(core == 0, heads_mine, heads_pair_other), pick(core == 0, heads_pair_other, heads_mine)]
    )
    heads_quad_other = swap_pairs(heads_pair, 2)
    heads_quad = jnp.concatenate(
        [pick(chip == 0, heads_pair, heads_quad_other), pick(chip == 0, heads_quad_other, heads_pair)]
    )
    w_out = w_output.reshape(row_count, q_width, w_output.shape[1])
    partial_out = jnp.einsum(
        "rtc,rco->to", heads_quad, w_out, preferred_element_type=jnp.float32
    ).astype(jnp.bfloat16)
    out_chunks = partial_out.reshape(col_count, shard_rows, -1)
    result = lax.dynamic_index_in_dim(out_chunks, col_at, 0, keepdims=False).astype(jnp.float32)
    for step in range(1, col_count):
        target = (col_at + step) % col_count
        sent = lax.dynamic_index_in_dim(out_chunks, target, 0, keepdims=False)
        result = result + shifted(sent, "col", step).astype(jnp.float32)
    return result.astype(jnp.bfloat16)


def solution(mesh):
    return jax.shard_map(
        on_device,
        mesh=mesh,
        in_specs=(
            P(("seq", "col"), "row"),
            P("row", "col"),
            P("row", "col"),
            P("row", "col"),
            P("col", "row"),
        ),
        out_specs=P(("seq", "col"), "row"),
        check_vma=False,
    )
```

```python
import jax
import jax.numpy as jnp
from jax import lax
from jax.sharding import PartitionSpec as P

HEADS = 32
KV_HEADS = 8
HEAD_DIM = 128


rope_base = 500000.0
masked_score = -1e30


def rotate(values, positions):
    half = HEAD_DIM // 2
    freqs = rope_base ** (-(jnp.arange(half, dtype=jnp.float32) * 2.0) / HEAD_DIM)
    angles = positions.astype(jnp.float32)[:, None] * freqs[None, :]
    cosine = jnp.concatenate([jnp.cos(angles), jnp.cos(angles)], axis=1)
    sine = jnp.concatenate([jnp.sin(angles), jnp.sin(angles)], axis=1)
    count = values.shape[0]
    heads = values.reshape(count, -1, HEAD_DIM)
    turned = jnp.concatenate([-heads[..., half:], heads[..., :half]], axis=-1)
    result = heads * cosine[:, None, :] + turned * sine[:, None, :]
    return result.reshape(count, -1)


def swap_pairs(value, flip):
    count = lax.axis_size("row")
    return lax.ppermute(value, "row", [(r, r ^ flip) for r in range(count)])


def shifted(value, axis, step):
    count = lax.axis_size(axis)
    return lax.ppermute(value, axis, [(i, (i + step) % count) for i in range(count)])


def pick(flag, first, second):
    return jnp.where(flag, first, second)


def on_device(tokens, w_query, w_key, w_value, w_output):
    shard_rows = tokens.shape[0]
    col_count = lax.axis_size("col")
    row_count = lax.axis_size("row")
    seq_count = lax.axis_size("seq")
    block_len = shard_rows * col_count
    key_len = block_len // 2
    seq_at = lax.axis_index("seq")
    row_at = lax.axis_index("row")
    core = row_at % 2
    chip = row_at // 2
    width_q = w_query.shape[1]
    width_kv = w_key.shape[1]
    local_kv = width_kv // HEAD_DIM
    assert row_count == 2 * local_kv
    q_width = width_q // row_count
    score_scale = HEAD_DIM ** (-0.5)

    col_at = lax.axis_index("col")
    pieces = [tokens] + [shifted(tokens, "col", step) for step in range(1, col_count)]
    order = (col_at - jnp.arange(col_count, dtype=jnp.int32)) % col_count
    block_tokens = jnp.take(jnp.stack(pieces), order, axis=0).reshape(block_len, -1)
    part_q = jnp.dot(block_tokens, w_query, preferred_element_type=jnp.float32)
    part_k = jnp.dot(block_tokens, w_key, preferred_element_type=jnp.float32)
    part_v = jnp.dot(block_tokens, w_value, preferred_element_type=jnp.float32)
    q_chunks = part_q.reshape(block_len, row_count, q_width).transpose(1, 0, 2)
    q_chunks = q_chunks.reshape(2, 2, block_len * q_width // HEAD_DIM, HEAD_DIM)

    def kv_chunks(part):
        split = part.reshape(2, key_len, local_kv, HEAD_DIM).transpose(2, 0, 1, 3)
        return split

    chunks = jnp.concatenate([q_chunks, kv_chunks(part_k), kv_chunks(part_v)], axis=2)
    keep_a = lax.dynamic_index_in_dim(chunks, core, axis=1, keepdims=False)
    send_a = lax.dynamic_index_in_dim(chunks, 1 - core, axis=1, keepdims=False)
    summed_a = keep_a + swap_pairs(send_a.astype(jnp.bfloat16), 1).astype(jnp.float32)
    keep_b = lax.dynamic_index_in_dim(summed_a, chip, axis=0, keepdims=False)
    send_b = lax.dynamic_index_in_dim(summed_a, 1 - chip, axis=0, keepdims=False)
    mine = keep_b + swap_pairs(send_b.astype(jnp.bfloat16), 2).astype(jnp.float32)

    q_rows = block_len * q_width // HEAD_DIM
    q_mine = mine[:q_rows].reshape(block_len, q_width)
    k_mine = mine[q_rows : q_rows + key_len]
    v_mine = mine[q_rows + key_len :]

    block_start = seq_at * block_len
    q_pos = block_start + jnp.arange(block_len, dtype=jnp.int32)
    k_offset = core * key_len + jnp.arange(key_len, dtype=jnp.int32)
    query = rotate(q_mine, q_pos).astype(jnp.bfloat16)
    keys = rotate(k_mine, block_start + k_offset).astype(jnp.bfloat16)
    kv_own = jnp.concatenate([keys, v_mine.astype(jnp.bfloat16)], axis=1)

    query_other = swap_pairs(query, 1)
    q_all = jnp.concatenate([query, query_other], axis=1)
    q_heads = q_all.reshape(block_len, -1, HEAD_DIM).transpose(1, 0, 2)
    n_heads = q_heads.shape[0]

    def attend(state, kv_rows, allowed):
        peak, total, summed = state
        key_blk = kv_rows[:, :HEAD_DIM]
        value_blk = kv_rows[:, HEAD_DIM:]
        scores = (
            jnp.einsum("hqd,kd->hqk", q_heads, key_blk, preferred_element_type=jnp.float32)
            * score_scale
        )
        scores = jnp.where(allowed[None], scores, masked_score)
        new_peak = jnp.maximum(peak, jnp.max(scores, axis=-1))
        weights = jnp.exp(scores - new_peak[..., None])
        factor = jnp.exp(peak - new_peak)
        total = total * factor + jnp.sum(weights, axis=-1)
        summed = summed * factor[..., None] + jnp.einsum(
            "hqk,kd->hqd",
            weights.astype(jnp.bfloat16),
            value_blk,
            preferred_element_type=jnp.float32,
        )
        return (new_peak, total, summed)

    state = (
        jnp.full((n_heads, block_len), masked_score, jnp.float32),
        jnp.zeros((n_heads, block_len), jnp.float32),
        jnp.zeros((n_heads, block_len, HEAD_DIM), jnp.float32),
    )
    own_pos = block_start + k_offset
    state = attend(state, kv_own, own_pos[None, :] <= q_pos[:, None])
    forward = [(s, (s + 1) % seq_count) for s in range(seq_count)]
    backward = [(s, (s - 1) % seq_count) for s in range(seq_count)]
    kv_fwd = kv_own
    kv_bwd = kv_own
    for step in range(1, seq_count // 2 + 1):
        kv_fwd = lax.ppermute(kv_fwd, "seq", forward)
        if step < seq_count // 2:
            kv_bwd = lax.ppermute(kv_bwd, "seq", backward)
        kv_fwd, kv_bwd, state = lax.optimization_barrier((kv_fwd, kv_bwd, state))
        fwd_pos = ((seq_at - step) % seq_count) * block_len + k_offset
        state = attend(state, kv_fwd, (fwd_pos < block_start)[None, :])
        if step < seq_count // 2:
            bwd_pos = ((seq_at + step) % seq_count) * block_len + k_offset
            state = attend(state, kv_bwd, (bwd_pos < block_start)[None, :])

    peak, total, summed = state
    other_peak, other_total, other_norm = swap_pairs(
        (peak, total, (summed / total[..., None]).astype(jnp.bfloat16)), 1
    )
    other_peak, other_total, other_norm = (
        jnp.roll(part, n_heads // 2, axis=0) for part in (other_peak, other_total, other_norm)
    )
    peak_all = jnp.maximum(peak, other_peak)
    factor_a = jnp.exp(peak - peak_all)
    factor_b = jnp.exp(other_peak - peak_all) * other_total
    total_all = total * factor_a + factor_b
    summed_all = summed * factor_a[..., None] + other_norm.astype(jnp.float32) * factor_b[..., None]
    heads_all = (summed_all / total_all[..., None]).astype(jnp.bfloat16)
    own = n_heads // 2
    heads_pair = pick(
        core == 0,
        heads_all,
        jnp.concatenate([heads_all[own:], heads_all[:own]], axis=0),
    )
    heads_pair = heads_pair.reshape(2, own, block_len, HEAD_DIM).transpose(0, 2, 1, 3)
    heads_pair = heads_pair.reshape(2, block_len, q_width)
    heads_quad_other = swap_pairs(heads_pair, 2)
    heads_quad = jnp.concatenate(
        [pick(chip == 0, heads_pair, heads_quad_other), pick(chip == 0, heads_quad_other, heads_pair)]
    )
    w_out = w_output.reshape(row_count, q_width, w_output.shape[1])
    partial_out = jnp.einsum(
        "rtc,rco->to", heads_quad, w_out, preferred_element_type=jnp.float32
    ).astype(jnp.bfloat16)
    out_chunks = partial_out.reshape(col_count, shard_rows, -1)
    result = lax.dynamic_index_in_dim(out_chunks, col_at, 0, keepdims=False).astype(jnp.float32)
    for step in range(1, col_count):
        target = (col_at + step) % col_count
        sent = lax.dynamic_index_in_dim(out_chunks, target, 0, keepdims=False)
        result = result + shifted(sent, "col", step).astype(jnp.float32)
    return result.astype(jnp.bfloat16)


def solution(mesh):
    return jax.shard_map(
        on_device,
        mesh=mesh,
        in_specs=(
            P(("seq", "col"), "row"),
            P("row", "col"),
            P("row", "col"),
            P("row", "col"),
            P("col", "row"),
        ),
        out_specs=P(("seq", "col"), "row"),
        check_vma=False,
    )
```

```python
import jax
import jax.numpy as jnp
from jax import lax
from jax.sharding import PartitionSpec as P

HEADS = 32
KV_HEADS = 8
HEAD_DIM = 128


rope_base = 500000.0
masked_score = -1e30


def rotate(values, positions):
    half = HEAD_DIM // 2
    freqs = rope_base ** (-(jnp.arange(half, dtype=jnp.float32) * 2.0) / HEAD_DIM)
    angles = positions.astype(jnp.float32)[:, None] * freqs[None, :]
    cosine = jnp.concatenate([jnp.cos(angles), jnp.cos(angles)], axis=1)
    sine = jnp.concatenate([jnp.sin(angles), jnp.sin(angles)], axis=1)
    count = values.shape[0]
    heads = values.reshape(count, -1, HEAD_DIM)
    turned = jnp.concatenate([-heads[..., half:], heads[..., :half]], axis=-1)
    result = heads * cosine[:, None, :] + turned * sine[:, None, :]
    return result.reshape(count, -1)


def swap_pairs(value, flip):
    count = lax.axis_size("row")
    return lax.ppermute(value, "row", [(r, r ^ flip) for r in range(count)])


def shifted(value, axis, step):
    count = lax.axis_size(axis)
    return lax.ppermute(value, axis, [(i, (i + step) % count) for i in range(count)])


def pick(flag, first, second):
    return jnp.where(flag, first, second)


def on_device(tokens, w_query, w_key, w_value, w_output):
    shard_rows = tokens.shape[0]
    col_count = lax.axis_size("col")
    row_count = lax.axis_size("row")
    seq_count = lax.axis_size("seq")
    block_len = shard_rows * col_count
    key_len = block_len // 2
    seq_at = lax.axis_index("seq")
    row_at = lax.axis_index("row")
    core = row_at % 2
    chip = row_at // 2
    width_q = w_query.shape[1]
    width_kv = w_key.shape[1]
    local_kv = width_kv // HEAD_DIM
    assert row_count == 2 * local_kv
    q_width = width_q // row_count
    score_scale = HEAD_DIM ** (-0.5)

    col_at = lax.axis_index("col")
    pieces = [tokens] + [shifted(tokens, "col", step) for step in range(1, col_count)]
    order = (col_at - jnp.arange(col_count, dtype=jnp.int32)) % col_count
    block_tokens = jnp.take(jnp.stack(pieces), order, axis=0).reshape(block_len, -1)
    part_q = jnp.dot(block_tokens, w_query, preferred_element_type=jnp.float32)
    part_k = jnp.dot(block_tokens, w_key, preferred_element_type=jnp.float32)
    part_v = jnp.dot(block_tokens, w_value, preferred_element_type=jnp.float32)
    q_chunks = part_q.reshape(block_len, row_count, q_width).transpose(1, 0, 2)
    q_chunks = q_chunks.reshape(2, 2, block_len * q_width // HEAD_DIM, HEAD_DIM)

    def kv_chunks(part):
        split = part.reshape(2, key_len, local_kv, HEAD_DIM).transpose(2, 0, 1, 3)
        return split

    chunks = jnp.concatenate([q_chunks, kv_chunks(part_k), kv_chunks(part_v)], axis=2)
    keep_a = lax.dynamic_index_in_dim(chunks, core, axis=1, keepdims=False)
    send_a = lax.dynamic_index_in_dim(chunks, 1 - core, axis=1, keepdims=False)
    summed_a = keep_a + swap_pairs(send_a.astype(jnp.bfloat16), 1).astype(jnp.float32)
    keep_b = lax.dynamic_index_in_dim(summed_a, chip, axis=0, keepdims=False)
    send_b = lax.dynamic_index_in_dim(summed_a, 1 - chip, axis=0, keepdims=False)
    mine = keep_b + swap_pairs(send_b.astype(jnp.bfloat16), 2).astype(jnp.float32)

    q_rows = block_len * q_width // HEAD_DIM
    q_mine = mine[:q_rows].reshape(block_len, q_width)
    k_mine = mine[q_rows : q_rows + key_len]
    v_mine = mine[q_rows + key_len :]

    block_start = seq_at * block_len
    q_pos = block_start + jnp.arange(block_len, dtype=jnp.int32)
    k_offset = core * key_len + jnp.arange(key_len, dtype=jnp.int32)
    query = rotate(q_mine, q_pos).astype(jnp.bfloat16)
    keys = rotate(k_mine, block_start + k_offset).astype(jnp.bfloat16)
    kv_own = jnp.concatenate([keys, v_mine.astype(jnp.bfloat16)], axis=1)

    query_other = swap_pairs(query, 1)
    q_all = jnp.concatenate([query, query_other], axis=1)
    q_heads = q_all.reshape(block_len, -1, HEAD_DIM).transpose(1, 0, 2)
    n_heads = q_heads.shape[0]

    def attend(state, kv_rows, allowed):
        peak, total, summed = state
        key_blk = kv_rows[:, :HEAD_DIM]
        value_blk = kv_rows[:, HEAD_DIM:]
        scores = (
            jnp.einsum("hqd,kd->hqk", q_heads, key_blk, preferred_element_type=jnp.float32)
            * score_scale
        )
        scores = jnp.where(allowed[None], scores, masked_score)
        new_peak = jnp.maximum(peak, jnp.max(scores, axis=-1))
        weights = jnp.exp(scores - new_peak[..., None])
        factor = jnp.exp(peak - new_peak)
        total = total * factor + jnp.sum(weights, axis=-1)
        summed = summed * factor[..., None] + jnp.einsum(
            "hqk,kd->hqd",
            weights.astype(jnp.bfloat16),
            value_blk,
            preferred_element_type=jnp.float32,
        )
        return (new_peak, total, summed)

    state = (
        jnp.full((n_heads, block_len), masked_score, jnp.float32),
        jnp.zeros((n_heads, block_len), jnp.float32),
        jnp.zeros((n_heads, block_len, HEAD_DIM), jnp.float32),
    )
    own_pos = block_start + k_offset
    state = attend(state, kv_own, own_pos[None, :] <= q_pos[:, None])
    half = seq_count // 2
    z_at = seq_at % half
    base = seq_at - z_at
    z_fwd = [(s, s - s % half + (s + 1) % half) for s in range(seq_count)]
    z_bwd = [(s, s - s % half + (s - 1) % half) for s in range(seq_count)]
    across = [(s, (s + half) % seq_count) for s in range(seq_count)]
    steps = half // 2
    pending = [(kv_own, seq_at)]
    kv_fwd = kv_own
    kv_bwd = kv_own
    for step in range(1, steps + 2):
        arrived = []
        if step <= steps:
            kv_fwd = lax.ppermute(kv_fwd, "seq", z_fwd)
            arrived.append((kv_fwd, base + (z_at - step) % half))
            if step < steps:
                kv_bwd = lax.ppermute(kv_bwd, "seq", z_bwd)
                arrived.append((kv_bwd, base + (z_at + step) % half))
        got = lax.ppermute(jnp.stack([kv for kv, _ in pending]), "seq", across)
        crossed = [(got[i], (block + half) % seq_count) for i, (_, block) in enumerate(pending)]
        incoming = arrived + crossed
        arrays, state = lax.optimization_barrier(([kv for kv, _ in incoming], state))
        for kv_rows, (_, block) in zip(arrays, incoming):
            state = attend(state, kv_rows, ((block * block_len + k_offset) < block_start)[None, :])
        pending = arrived

    peak, total, summed = state
    other_peak, other_total, other_norm = swap_pairs(
        (peak, total, (summed / total[..., None]).astype(jnp.bfloat16)), 1
    )
    other_peak, other_total, other_norm = (
        jnp.roll(part, n_heads // 2, axis=0) for part in (other_peak, other_total, other_norm)
    )
    peak_all = jnp.maximum(peak, other_peak)
    factor_a = jnp.exp(peak - peak_all)
    factor_b = jnp.exp(other_peak - peak_all) * other_total
    total_all = total * factor_a + factor_b
    summed_all = summed * factor_a[..., None] + other_norm.astype(jnp.float32) * factor_b[..., None]
    heads_all = (summed_all / total_all[..., None]).astype(jnp.bfloat16)
    own = n_heads // 2
    heads_pair = pick(
        core == 0,
        heads_all,
        jnp.concatenate([heads_all[own:], heads_all[:own]], axis=0),
    )
    heads_pair = heads_pair.reshape(2, own, block_len, HEAD_DIM).transpose(0, 2, 1, 3)
    heads_pair = heads_pair.reshape(2, block_len, q_width)
    heads_quad_other = swap_pairs(heads_pair, 2)
    heads_quad = jnp.concatenate(
        [pick(chip == 0, heads_pair, heads_quad_other), pick(chip == 0, heads_quad_other, heads_pair)]
    )
    w_out = w_output.reshape(row_count, q_width, w_output.shape[1])
    partial_out = jnp.einsum(
        "rtc,rco->to", heads_quad, w_out, preferred_element_type=jnp.float32
    ).astype(jnp.bfloat16)
    out_chunks = partial_out.reshape(col_count, shard_rows, -1)
    result = lax.dynamic_index_in_dim(out_chunks, col_at, 0, keepdims=False).astype(jnp.float32)
    for step in range(1, col_count):
        target = (col_at + step) % col_count
        sent = lax.dynamic_index_in_dim(out_chunks, target, 0, keepdims=False)
        result = result + shifted(sent, "col", step).astype(jnp.float32)
    return result.astype(jnp.bfloat16)


def solution(mesh):
    return jax.shard_map(
        on_device,
        mesh=mesh,
        in_specs=(
            P(("seq", "col"), "row"),
            P("row", "col"),
            P("row", "col"),
            P("row", "col"),
            P("col", "row"),
        ),
        out_specs=P(("seq", "col"), "row"),
        check_vma=False,
    )
```

```python
import jax
import jax.numpy as jnp
from jax import lax
from jax.sharding import PartitionSpec as P

HEADS = 32
KV_HEADS = 8
HEAD_DIM = 128


rope_base = 500000.0
masked_score = -1e30


def rotate(values, positions):
    half = HEAD_DIM // 2
    freqs = rope_base ** (-(jnp.arange(half, dtype=jnp.float32) * 2.0) / HEAD_DIM)
    angles = positions.astype(jnp.float32)[:, None] * freqs[None, :]
    cosine = jnp.concatenate([jnp.cos(angles), jnp.cos(angles)], axis=1)
    sine = jnp.concatenate([jnp.sin(angles), jnp.sin(angles)], axis=1)
    count = values.shape[0]
    heads = values.reshape(count, -1, HEAD_DIM)
    turned = jnp.concatenate([-heads[..., half:], heads[..., :half]], axis=-1)
    result = heads * cosine[:, None, :] + turned * sine[:, None, :]
    return result.reshape(count, -1)


def swap_pairs(value, flip):
    count = lax.axis_size("row")
    return lax.ppermute(value, "row", [(r, r ^ flip) for r in range(count)])


def shifted(value, axis, step):
    count = lax.axis_size(axis)
    return lax.ppermute(value, axis, [(i, (i + step) % count) for i in range(count)])


def pick(flag, first, second):
    return jnp.where(flag, first, second)


def on_device(tokens, w_query, w_key, w_value, w_output):
    shard_rows = tokens.shape[0]
    col_count = lax.axis_size("col")
    row_count = lax.axis_size("row")
    seq_count = lax.axis_size("seq")
    block_len = shard_rows * col_count
    key_len = block_len // 2
    seq_at = lax.axis_index("seq")
    row_at = lax.axis_index("row")
    core = row_at % 2
    chip = row_at // 2
    width_q = w_query.shape[1]
    width_kv = w_key.shape[1]
    local_kv = width_kv // HEAD_DIM
    assert row_count == 2 * local_kv
    q_width = width_q // row_count
    score_scale = HEAD_DIM ** (-0.5)

    col_at = lax.axis_index("col")
    pieces = [tokens] + [shifted(tokens, "col", step) for step in range(1, col_count)]
    order = (col_at - jnp.arange(col_count, dtype=jnp.int32)) % col_count
    block_tokens = jnp.take(jnp.stack(pieces), order, axis=0).reshape(block_len, -1)
    part_q = jnp.dot(block_tokens, w_query, preferred_element_type=jnp.float32)
    part_k = jnp.dot(block_tokens, w_key, preferred_element_type=jnp.float32)
    part_v = jnp.dot(block_tokens, w_value, preferred_element_type=jnp.float32)
    q_chunks = part_q.reshape(block_len, row_count, q_width).transpose(1, 0, 2)
    q_chunks = q_chunks.reshape(2, 2, block_len * q_width // HEAD_DIM, HEAD_DIM)

    def kv_chunks(part):
        split = part.reshape(2, key_len, local_kv, HEAD_DIM).transpose(2, 0, 1, 3)
        return split

    chunks = jnp.concatenate([q_chunks, kv_chunks(part_k), kv_chunks(part_v)], axis=2)
    keep_a = lax.dynamic_index_in_dim(chunks, core, axis=1, keepdims=False)
    send_a = lax.dynamic_index_in_dim(chunks, 1 - core, axis=1, keepdims=False)
    summed_a = keep_a + swap_pairs(send_a.astype(jnp.bfloat16), 1).astype(jnp.float32)
    keep_b = lax.dynamic_index_in_dim(summed_a, chip, axis=0, keepdims=False)
    send_b = lax.dynamic_index_in_dim(summed_a, 1 - chip, axis=0, keepdims=False)
    mine = keep_b + swap_pairs(send_b.astype(jnp.bfloat16), 2).astype(jnp.float32)

    q_rows = block_len * q_width // HEAD_DIM
    q_mine = mine[:q_rows].reshape(block_len, q_width)
    k_mine = mine[q_rows : q_rows + key_len]
    v_mine = mine[q_rows + key_len :]

    block_start = seq_at * block_len
    q_pos = block_start + jnp.arange(block_len, dtype=jnp.int32)
    k_offset = core * key_len + jnp.arange(key_len, dtype=jnp.int32)
    query = rotate(q_mine, q_pos).astype(jnp.bfloat16)
    keys = rotate(k_mine, block_start + k_offset).astype(jnp.bfloat16)
    kv_own = jnp.concatenate([keys, v_mine.astype(jnp.bfloat16)], axis=1)

    query_other = swap_pairs(query, 1)
    q_all = jnp.concatenate([query, query_other], axis=1)
    q_heads = q_all.reshape(block_len, -1, HEAD_DIM).transpose(1, 0, 2)
    n_heads = q_heads.shape[0]

    def attend(state, kv_rows, allowed):
        peak, total, summed = state
        key_blk = kv_rows[:, :HEAD_DIM]
        value_blk = kv_rows[:, HEAD_DIM:]
        scores = (
            jnp.einsum("hqd,kd->hqk", q_heads, key_blk, preferred_element_type=jnp.float32)
            * score_scale
        )
        scores = jnp.where(allowed[None], scores, masked_score)
        new_peak = jnp.maximum(peak, jnp.max(scores, axis=-1))
        weights = jnp.exp(scores - new_peak[..., None])
        factor = jnp.exp(peak - new_peak)
        total = total * factor + jnp.sum(weights, axis=-1)
        summed = summed * factor[..., None] + jnp.einsum(
            "hqk,kd->hqd",
            weights.astype(jnp.bfloat16),
            value_blk,
            preferred_element_type=jnp.float32,
        )
        return (new_peak, total, summed)

    state = (
        jnp.full((n_heads, block_len), masked_score, jnp.float32),
        jnp.zeros((n_heads, block_len), jnp.float32),
        jnp.zeros((n_heads, block_len, HEAD_DIM), jnp.float32),
    )
    own_pos = block_start + k_offset
    state = attend(state, kv_own, own_pos[None, :] <= q_pos[:, None])
    half = seq_count // 2
    z_at = seq_at % half
    base = seq_at - z_at
    z_fwd = [(s, s - s % half + (s + 1) % half) for s in range(seq_count)]
    z_bwd = [(s, s - s % half + (s - 1) % half) for s in range(seq_count)]
    across = [(s, (s + half) % seq_count) for s in range(seq_count)]
    steps = half // 2
    pending = [(kv_own, seq_at)]
    kv_fwd = kv_own
    kv_bwd = kv_own
    for step in range(1, steps + 2):
        arrived = []
        if step <= steps:
            kv_fwd = lax.ppermute(kv_fwd, "seq", z_fwd)
            arrived.append((kv_fwd, base + (z_at - step) % half))
            if step < steps:
                kv_bwd = lax.ppermute(kv_bwd, "seq", z_bwd)
                arrived.append((kv_bwd, base + (z_at + step) % half))
        got = lax.ppermute(jnp.stack([kv for kv, _ in pending]), "seq", across)
        crossed = [(got[i], (block + half) % seq_count) for i, (_, block) in enumerate(pending)]
        incoming = arrived + crossed
        arrays, state = lax.optimization_barrier(([kv for kv, _ in incoming], state))
        kv_step = jnp.concatenate(arrays, axis=0)
        step_pos = jnp.concatenate([block * block_len + k_offset for _, block in incoming])
        state = attend(state, kv_step, (step_pos < block_start)[None, :])
        pending = arrived

    peak, total, summed = state
    other_peak, other_total, other_norm = swap_pairs(
        (peak, total, (summed / total[..., None]).astype(jnp.bfloat16)), 1
    )
    other_peak, other_total, other_norm = (
        jnp.roll(part, n_heads // 2, axis=0) for part in (other_peak, other_total, other_norm)
    )
    peak_all = jnp.maximum(peak, other_peak)
    factor_a = jnp.exp(peak - peak_all)
    factor_b = jnp.exp(other_peak - peak_all) * other_total
    total_all = total * factor_a + factor_b
    summed_all = summed * factor_a[..., None] + other_norm.astype(jnp.float32) * factor_b[..., None]
    heads_all = (summed_all / total_all[..., None]).astype(jnp.bfloat16)
    own = n_heads // 2
    heads_pair = pick(
        core == 0,
        heads_all,
        jnp.concatenate([heads_all[own:], heads_all[:own]], axis=0),
    )
    heads_pair = heads_pair.reshape(2, own, block_len, HEAD_DIM).transpose(0, 2, 1, 3)
    heads_pair = heads_pair.reshape(2, block_len, q_width)
    heads_quad_other = swap_pairs(heads_pair, 2)
    heads_quad = jnp.concatenate(
        [pick(chip == 0, heads_pair, heads_quad_other), pick(chip == 0, heads_quad_other, heads_pair)]
    )
    w_out = w_output.reshape(row_count, q_width, w_output.shape[1])
    partial_out = jnp.einsum(
        "rtc,rco->to", heads_quad, w_out, preferred_element_type=jnp.float32
    ).astype(jnp.bfloat16)
    out_chunks = partial_out.reshape(col_count, shard_rows, -1)
    result = lax.dynamic_index_in_dim(out_chunks, col_at, 0, keepdims=False).astype(jnp.float32)
    for step in range(1, col_count):
        target = (col_at + step) % col_count
        sent = lax.dynamic_index_in_dim(out_chunks, target, 0, keepdims=False)
        result = result + shifted(sent, "col", step).astype(jnp.float32)
    return result.astype(jnp.bfloat16)


def solution(mesh):
    return jax.shard_map(
        on_device,
        mesh=mesh,
        in_specs=(
            P(("seq", "col"), "row"),
            P("row", "col"),
            P("row", "col"),
            P("row", "col"),
            P("col", "row"),
        ),
        out_specs=P(("seq", "col"), "row"),
        check_vma=False,
    )
```

```python
import jax
import jax.numpy as jnp
from jax import lax
from jax.sharding import PartitionSpec as P

HEADS = 32
KV_HEADS = 8
HEAD_DIM = 128


rope_base = 500000.0
masked_score = -1e30


def rotate(values, positions):
    half = HEAD_DIM // 2
    freqs = rope_base ** (-(jnp.arange(half, dtype=jnp.float32) * 2.0) / HEAD_DIM)
    angles = positions.astype(jnp.float32)[:, None] * freqs[None, :]
    cosine = jnp.concatenate([jnp.cos(angles), jnp.cos(angles)], axis=1)
    sine = jnp.concatenate([jnp.sin(angles), jnp.sin(angles)], axis=1)
    count = values.shape[0]
    heads = values.reshape(count, -1, HEAD_DIM)
    turned = jnp.concatenate([-heads[..., half:], heads[..., :half]], axis=-1)
    result = heads * cosine[:, None, :] + turned * sine[:, None, :]
    return result.reshape(count, -1)


def swap_pairs(value, flip):
    count = lax.axis_size("row")
    return lax.ppermute(value, "row", [(r, r ^ flip) for r in range(count)])


def shifted(value, axis, step):
    count = lax.axis_size(axis)
    return lax.ppermute(value, axis, [(i, (i + step) % count) for i in range(count)])


def pick(flag, first, second):
    return jnp.where(flag, first, second)


def on_device(tokens, w_query, w_key, w_value, w_output):
    shard_rows = tokens.shape[0]
    col_count = lax.axis_size("col")
    row_count = lax.axis_size("row")
    seq_count = lax.axis_size("seq")
    block_len = shard_rows * col_count
    key_len = block_len // 2
    seq_at = lax.axis_index("seq")
    row_at = lax.axis_index("row")
    core = row_at % 2
    chip = row_at // 2
    width_q = w_query.shape[1]
    width_kv = w_key.shape[1]
    local_kv = width_kv // HEAD_DIM
    assert row_count == 2 * local_kv
    q_width = width_q // row_count
    score_scale = HEAD_DIM ** (-0.5)

    col_at = lax.axis_index("col")
    pieces = [tokens] + [shifted(tokens, "col", step) for step in range(1, col_count)]
    order = (col_at - jnp.arange(col_count, dtype=jnp.int32)) % col_count
    block_tokens = jnp.take(jnp.stack(pieces), order, axis=0).reshape(block_len, -1)
    part_q = jnp.dot(block_tokens, w_query, preferred_element_type=jnp.float32)
    part_k = jnp.dot(block_tokens, w_key, preferred_element_type=jnp.float32)
    part_v = jnp.dot(block_tokens, w_value, preferred_element_type=jnp.float32)
    q_chunks = part_q.reshape(block_len, row_count, q_width).transpose(1, 0, 2)
    q_chunks = q_chunks.reshape(2, 2, block_len * q_width // HEAD_DIM, HEAD_DIM)

    def kv_chunks(part):
        split = part.reshape(2, key_len, local_kv, HEAD_DIM).transpose(2, 0, 1, 3)
        return split

    chunks = jnp.concatenate([q_chunks, kv_chunks(part_k), kv_chunks(part_v)], axis=2)
    keep_a = lax.dynamic_index_in_dim(chunks, core, axis=1, keepdims=False)
    send_a = lax.dynamic_index_in_dim(chunks, 1 - core, axis=1, keepdims=False)
    summed_a = keep_a + swap_pairs(send_a.astype(jnp.bfloat16), 1).astype(jnp.float32)
    keep_b = lax.dynamic_index_in_dim(summed_a, chip, axis=0, keepdims=False)
    send_b = lax.dynamic_index_in_dim(summed_a, 1 - chip, axis=0, keepdims=False)
    mine = keep_b + swap_pairs(send_b.astype(jnp.bfloat16), 2).astype(jnp.float32)

    q_rows = block_len * q_width // HEAD_DIM
    q_mine = mine[:q_rows].reshape(block_len, q_width)
    k_mine = mine[q_rows : q_rows + key_len]
    v_mine = mine[q_rows + key_len :]

    block_start = seq_at * block_len
    q_pos = block_start + jnp.arange(block_len, dtype=jnp.int32)
    k_offset = core * key_len + jnp.arange(key_len, dtype=jnp.int32)
    query = rotate(q_mine, q_pos).astype(jnp.bfloat16)
    keys = rotate(k_mine, block_start + k_offset).astype(jnp.bfloat16)
    kv_own = jnp.concatenate([keys, v_mine.astype(jnp.bfloat16)], axis=1)

    query_other = swap_pairs(query, 1)
    q_all = jnp.concatenate([query, query_other], axis=1)
    q_heads = q_all.reshape(block_len, -1, HEAD_DIM).transpose(1, 0, 2)
    n_heads = q_heads.shape[0]

    def attend(state, kv_rows, allowed):
        peak, total, summed = state
        key_blk = kv_rows[:, :HEAD_DIM]
        value_blk = kv_rows[:, HEAD_DIM:]
        scores = (
            jnp.einsum("hqd,kd->hqk", q_heads, key_blk, preferred_element_type=jnp.float32)
            * score_scale
        )
        scores = jnp.where(allowed[None], scores, masked_score)
        new_peak = jnp.maximum(peak, jnp.max(scores, axis=-1))
        weights = jnp.exp(scores - new_peak[..., None])
        factor = jnp.exp(peak - new_peak)
        total = total * factor + jnp.sum(weights, axis=-1)
        summed = summed * factor[..., None] + jnp.einsum(
            "hqk,kd->hqd",
            weights.astype(jnp.bfloat16),
            value_blk,
            preferred_element_type=jnp.float32,
        )
        return (new_peak, total, summed)

    state = (
        jnp.full((n_heads, block_len), masked_score, jnp.float32),
        jnp.zeros((n_heads, block_len), jnp.float32),
        jnp.zeros((n_heads, block_len, HEAD_DIM), jnp.float32),
    )
    own_pos = block_start + k_offset
    state = attend(state, kv_own, own_pos[None, :] <= q_pos[:, None])
    half = seq_count // 2
    z_at = seq_at % half
    base = seq_at - z_at
    z_fwd = [(s, s - s % half + (s + 1) % half) for s in range(seq_count)]
    z_bwd = [(s, s - s % half + (s - 1) % half) for s in range(seq_count)]
    across = [(s, (s + half) % seq_count) for s in range(seq_count)]
    steps = half // 2
    pending = [(kv_own, seq_at)]
    kv_fwd = kv_own
    kv_bwd = kv_own
    for step in range(1, steps + 2):
        arrived = []
        if step <= steps:
            kv_fwd = lax.ppermute(kv_fwd, "seq", z_fwd)
            arrived.append((kv_fwd, base + (z_at - step) % half))
            if step < steps:
                kv_bwd = lax.ppermute(kv_bwd, "seq", z_bwd)
                arrived.append((kv_bwd, base + (z_at + step) % half))
        got = lax.ppermute(jnp.stack([kv for kv, _ in pending]), "seq", across)
        crossed = [(got[i], (block + half) % seq_count) for i, (_, block) in enumerate(pending)]
        incoming = arrived + crossed
        arrays, state = lax.optimization_barrier(([kv for kv, _ in incoming], state))
        kv_step = jnp.concatenate(arrays, axis=0)
        step_pos = jnp.concatenate([block * block_len + k_offset for _, block in incoming])
        state = attend(state, kv_step, (step_pos < block_start)[None, :])
        pending = arrived

    peak, total, summed = state
    other_peak, other_total, other_norm = swap_pairs(
        (peak, total, (summed / total[..., None]).astype(jnp.bfloat16)), 1
    )
    other_peak, other_total, other_norm = (
        jnp.roll(part, n_heads // 2, axis=0) for part in (other_peak, other_total, other_norm)
    )
    peak_all = jnp.maximum(peak, other_peak)
    factor_a = jnp.exp(peak - peak_all)
    factor_b = jnp.exp(other_peak - peak_all) * other_total
    total_all = total * factor_a + factor_b
    summed_all = summed * factor_a[..., None] + other_norm.astype(jnp.float32) * factor_b[..., None]
    heads_all = (summed_all / total_all[..., None]).astype(jnp.bfloat16)
    own = n_heads // 2
    heads_pair = pick(
        core == 0,
        heads_all,
        jnp.concatenate([heads_all[own:], heads_all[:own]], axis=0),
    )
    heads_pair = heads_pair.reshape(2, own, block_len, HEAD_DIM).transpose(0, 2, 1, 3)
    heads_pair = heads_pair.reshape(2, block_len, q_width)
    got_x = swap_pairs(lax.dynamic_index_in_dim(heads_pair, core, 0, keepdims=False), 2)
    got_partner = swap_pairs(got_x, 1)
    heads_quad_other = jnp.stack(
        [pick(core == 0, got_x, got_partner), pick(core == 0, got_partner, got_x)]
    )
    heads_quad = jnp.concatenate(
        [pick(chip == 0, heads_pair, heads_quad_other), pick(chip == 0, heads_quad_other, heads_pair)]
    )
    w_out = w_output.reshape(row_count, q_width, w_output.shape[1])
    partial_out = jnp.einsum(
        "rtc,rco->to", heads_quad, w_out, preferred_element_type=jnp.float32
    ).astype(jnp.bfloat16)
    out_chunks = partial_out.reshape(col_count, shard_rows, -1)
    result = lax.dynamic_index_in_dim(out_chunks, col_at, 0, keepdims=False).astype(jnp.float32)
    for step in range(1, col_count):
        target = (col_at + step) % col_count
        sent = lax.dynamic_index_in_dim(out_chunks, target, 0, keepdims=False)
        result = result + shifted(sent, "col", step).astype(jnp.float32)
    return result.astype(jnp.bfloat16)


def solution(mesh):
    return jax.shard_map(
        on_device,
        mesh=mesh,
        in_specs=(
            P(("seq", "col"), "row"),
            P("row", "col"),
            P("row", "col"),
            P("row", "col"),
            P("col", "row"),
        ),
        out_specs=P(("seq", "col"), "row"),
        check_vma=False,
    )
```

```python
import jax
import jax.numpy as jnp
from jax import lax
from jax.sharding import PartitionSpec as P

HEADS = 32
KV_HEADS = 8
HEAD_DIM = 128


rope_base = 500000.0
masked_score = -1e30


def rotate(values, positions):
    half = HEAD_DIM // 2
    freqs = rope_base ** (-(jnp.arange(half, dtype=jnp.float32) * 2.0) / HEAD_DIM)
    angles = positions.astype(jnp.float32)[:, None] * freqs[None, :]
    cosine = jnp.concatenate([jnp.cos(angles), jnp.cos(angles)], axis=1)
    sine = jnp.concatenate([jnp.sin(angles), jnp.sin(angles)], axis=1)
    count = values.shape[0]
    heads = values.reshape(count, -1, HEAD_DIM)
    turned = jnp.concatenate([-heads[..., half:], heads[..., :half]], axis=-1)
    result = heads * cosine[:, None, :] + turned * sine[:, None, :]
    return result.reshape(count, -1)


def swap_pairs(value, flip):
    count = lax.axis_size("row")
    return lax.ppermute(value, "row", [(r, r ^ flip) for r in range(count)])


def shifted(value, axis, step):
    count = lax.axis_size(axis)
    return lax.ppermute(value, axis, [(i, (i + step) % count) for i in range(count)])


def pick(flag, first, second):
    return jnp.where(flag, first, second)


def on_device(tokens, w_query, w_key, w_value, w_output):
    shard_rows = tokens.shape[0]
    col_count = lax.axis_size("col")
    row_count = lax.axis_size("row")
    seq_count = lax.axis_size("seq")
    block_len = shard_rows * col_count
    key_len = block_len // 2
    seq_at = lax.axis_index("seq")
    row_at = lax.axis_index("row")
    core = row_at % 2
    chip = row_at // 2
    width_q = w_query.shape[1]
    width_kv = w_key.shape[1]
    local_kv = width_kv // HEAD_DIM
    assert row_count == 2 * local_kv
    q_width = width_q // row_count
    score_scale = HEAD_DIM ** (-0.5)

    col_at = lax.axis_index("col")
    pieces = [tokens] + [shifted(tokens, "col", step) for step in range(1, col_count)]
    order = (col_at - jnp.arange(col_count, dtype=jnp.int32)) % col_count
    block_tokens = jnp.take(jnp.stack(pieces), order, axis=0).reshape(block_len, -1)
    part_q = jnp.dot(block_tokens, w_query, preferred_element_type=jnp.float32)
    part_k = jnp.dot(block_tokens, w_key, preferred_element_type=jnp.float32)
    part_v = jnp.dot(block_tokens, w_value, preferred_element_type=jnp.float32)
    q_chunks = part_q.reshape(block_len, row_count, q_width).transpose(1, 0, 2)
    q_chunks = q_chunks.reshape(2, 2, block_len * q_width // HEAD_DIM, HEAD_DIM)

    def kv_chunks(part):
        split = part.reshape(2, key_len, local_kv, HEAD_DIM).transpose(2, 0, 1, 3)
        return split

    def reduce_over_row(chunks):
        keep_a = lax.dynamic_index_in_dim(chunks, core, axis=1, keepdims=False)
        send_a = lax.dynamic_index_in_dim(chunks, 1 - core, axis=1, keepdims=False)
        summed_a = keep_a + swap_pairs(send_a.astype(jnp.bfloat16), 1).astype(jnp.float32)
        keep_b = lax.dynamic_index_in_dim(summed_a, chip, axis=0, keepdims=False)
        send_b = lax.dynamic_index_in_dim(summed_a, 1 - chip, axis=0, keepdims=False)
        return keep_b + swap_pairs(send_b.astype(jnp.bfloat16), 2).astype(jnp.float32)

    kv_mine = reduce_over_row(jnp.concatenate([kv_chunks(part_k), kv_chunks(part_v)], axis=2))
    q_mine = reduce_over_row(q_chunks).reshape(block_len, q_width)
    k_mine = kv_mine[:key_len]
    v_mine = kv_mine[key_len:]

    block_start = seq_at * block_len
    q_pos = block_start + jnp.arange(block_len, dtype=jnp.int32)
    k_offset = core * key_len + jnp.arange(key_len, dtype=jnp.int32)
    query = rotate(q_mine, q_pos).astype(jnp.bfloat16)
    keys = rotate(k_mine, block_start + k_offset).astype(jnp.bfloat16)
    kv_own = jnp.concatenate([keys, v_mine.astype(jnp.bfloat16)], axis=1)

    query_other = swap_pairs(query, 1)
    q_all = jnp.concatenate([query, query_other], axis=1)
    q_heads = q_all.reshape(block_len, -1, HEAD_DIM).transpose(1, 0, 2)
    n_heads = q_heads.shape[0]

    def attend(state, kv_rows, allowed):
        peak, total, summed = state
        key_blk = kv_rows[:, :HEAD_DIM]
        value_blk = kv_rows[:, HEAD_DIM:]
        scores = (
            jnp.einsum("hqd,kd->hqk", q_heads, key_blk, preferred_element_type=jnp.float32)
            * score_scale
        )
        scores = jnp.where(allowed[None], scores, masked_score)
        new_peak = jnp.maximum(peak, jnp.max(scores, axis=-1))
        weights = jnp.exp(scores - new_peak[..., None])
        factor = jnp.exp(peak - new_peak)
        total = total * factor + jnp.sum(weights, axis=-1)
        summed = summed * factor[..., None] + jnp.einsum(
            "hqk,kd->hqd",
            weights.astype(jnp.bfloat16),
            value_blk,
            preferred_element_type=jnp.float32,
        )
        return (new_peak, total, summed)

    state = (
        jnp.full((n_heads, block_len), masked_score, jnp.float32),
        jnp.zeros((n_heads, block_len), jnp.float32),
        jnp.zeros((n_heads, block_len, HEAD_DIM), jnp.float32),
    )
    own_pos = block_start + k_offset
    state = attend(state, kv_own, own_pos[None, :] <= q_pos[:, None])
    half = seq_count // 2
    z_at = seq_at % half
    base = seq_at - z_at
    z_fwd = [(s, s - s % half + (s + 1) % half) for s in range(seq_count)]
    z_bwd = [(s, s - s % half + (s - 1) % half) for s in range(seq_count)]
    across = [(s, (s + half) % seq_count) for s in range(seq_count)]
    steps = half // 2
    pending = [(kv_own, seq_at)]
    kv_fwd = kv_own
    kv_bwd = kv_own
    for step in range(1, steps + 2):
        arrived = []
        if step <= steps:
            kv_fwd = lax.ppermute(kv_fwd, "seq", z_fwd)
            arrived.append((kv_fwd, base + (z_at - step) % half))
            if step < steps:
                kv_bwd = lax.ppermute(kv_bwd, "seq", z_bwd)
                arrived.append((kv_bwd, base + (z_at + step) % half))
        got = lax.ppermute(jnp.stack([kv for kv, _ in pending]), "seq", across)
        crossed = [(got[i], (block + half) % seq_count) for i, (_, block) in enumerate(pending)]
        incoming = arrived + crossed
        arrays, state = lax.optimization_barrier(([kv for kv, _ in incoming], state))
        kv_step = jnp.concatenate(arrays, axis=0)
        step_pos = jnp.concatenate([block * block_len + k_offset for _, block in incoming])
        state = attend(state, kv_step, (step_pos < block_start)[None, :])
        pending = arrived

    peak, total, summed = state
    other_peak, other_total, other_norm = swap_pairs(
        (peak, total, (summed / total[..., None]).astype(jnp.bfloat16)), 1
    )
    other_peak, other_total, other_norm = (
        jnp.roll(part, n_heads // 2, axis=0) for part in (other_peak, other_total, other_norm)
    )
    peak_all = jnp.maximum(peak, other_peak)
    factor_a = jnp.exp(peak - peak_all)
    factor_b = jnp.exp(other_peak - peak_all) * other_total
    total_all = total * factor_a + factor_b
    summed_all = summed * factor_a[..., None] + other_norm.astype(jnp.float32) * factor_b[..., None]
    heads_all = (summed_all / total_all[..., None]).astype(jnp.bfloat16)
    own = n_heads // 2
    heads_pair = pick(
        core == 0,
        heads_all,
        jnp.concatenate([heads_all[own:], heads_all[:own]], axis=0),
    )
    heads_pair = heads_pair.reshape(2, own, block_len, HEAD_DIM).transpose(0, 2, 1, 3)
    heads_pair = heads_pair.reshape(2, block_len, q_width)
    got_x = swap_pairs(lax.dynamic_index_in_dim(heads_pair, core, 0, keepdims=False), 2)
    got_partner = swap_pairs(got_x, 1)
    heads_quad_other = jnp.stack(
        [pick(core == 0, got_x, got_partner), pick(core == 0, got_partner, got_x)]
    )
    heads_quad = jnp.concatenate(
        [pick(chip == 0, heads_pair, heads_quad_other), pick(chip == 0, heads_quad_other, heads_pair)]
    )
    w_out = w_output.reshape(row_count, q_width, w_output.shape[1])
    partial_out = jnp.einsum(
        "rtc,rco->to", heads_quad, w_out, preferred_element_type=jnp.float32
    ).astype(jnp.bfloat16)
    out_chunks = partial_out.reshape(col_count, shard_rows, -1)
    result = lax.dynamic_index_in_dim(out_chunks, col_at, 0, keepdims=False).astype(jnp.float32)
    for step in range(1, col_count):
        target = (col_at + step) % col_count
        sent = lax.dynamic_index_in_dim(out_chunks, target, 0, keepdims=False)
        result = result + shifted(sent, "col", step).astype(jnp.float32)
    return result.astype(jnp.bfloat16)


def solution(mesh):
    return jax.shard_map(
        on_device,
        mesh=mesh,
        in_specs=(
            P(("seq", "col"), "row"),
            P("row", "col"),
            P("row", "col"),
            P("row", "col"),
            P("col", "row"),
        ),
        out_specs=P(("seq", "col"), "row"),
        check_vma=False,
    )
```

```python
import jax
import jax.numpy as jnp
from jax import lax
from jax.sharding import PartitionSpec as P

HEADS = 32
KV_HEADS = 8
HEAD_DIM = 128


rope_base = 500000.0
masked_score = -1e30


def rotate(values, positions):
    half = HEAD_DIM // 2
    freqs = rope_base ** (-(jnp.arange(half, dtype=jnp.float32) * 2.0) / HEAD_DIM)
    angles = positions.astype(jnp.float32)[:, None] * freqs[None, :]
    cosine = jnp.concatenate([jnp.cos(angles), jnp.cos(angles)], axis=1)
    sine = jnp.concatenate([jnp.sin(angles), jnp.sin(angles)], axis=1)
    count = values.shape[0]
    heads = values.reshape(count, -1, HEAD_DIM)
    turned = jnp.concatenate([-heads[..., half:], heads[..., :half]], axis=-1)
    result = heads * cosine[:, None, :] + turned * sine[:, None, :]
    return result.reshape(count, -1)


def swap_pairs(value, flip):
    count = lax.axis_size("row")
    return lax.ppermute(value, "row", [(r, r ^ flip) for r in range(count)])


def shifted(value, axis, step):
    count = lax.axis_size(axis)
    return lax.ppermute(value, axis, [(i, (i + step) % count) for i in range(count)])


def pick(flag, first, second):
    return jnp.where(flag, first, second)


def on_device(tokens, w_query, w_key, w_value, w_output):
    shard_rows = tokens.shape[0]
    col_count = lax.axis_size("col")
    row_count = lax.axis_size("row")
    seq_count = lax.axis_size("seq")
    block_len = shard_rows * col_count
    key_len = block_len // 2
    seq_at = lax.axis_index("seq")
    row_at = lax.axis_index("row")
    core = row_at % 2
    chip = row_at // 2
    width_q = w_query.shape[1]
    width_kv = w_key.shape[1]
    local_kv = width_kv // HEAD_DIM
    assert row_count == 2 * local_kv
    q_width = width_q // row_count
    score_scale = HEAD_DIM ** (-0.5)

    col_at = lax.axis_index("col")
    pieces = [tokens] + [shifted(tokens, "col", step) for step in range(1, col_count)]
    order = (col_at - jnp.arange(col_count, dtype=jnp.int32)) % col_count
    block_tokens = jnp.take(jnp.stack(pieces), order, axis=0).reshape(block_len, -1)
    part_q = jnp.dot(block_tokens, w_query, preferred_element_type=jnp.float32)
    part_k = jnp.dot(block_tokens, w_key, preferred_element_type=jnp.float32)
    part_v = jnp.dot(block_tokens, w_value, preferred_element_type=jnp.float32)
    q_chunks = part_q.reshape(block_len, row_count, q_width).transpose(1, 0, 2)
    q_chunks = q_chunks.reshape(2, 2, block_len * q_width // HEAD_DIM, HEAD_DIM)

    def kv_chunks(part):
        split = part.reshape(2, key_len, local_kv, HEAD_DIM).transpose(2, 0, 1, 3)
        return split

    chunks = jnp.concatenate([q_chunks, kv_chunks(part_k), kv_chunks(part_v)], axis=2)
    keep_a = lax.dynamic_index_in_dim(chunks, core, axis=1, keepdims=False)
    send_a = lax.dynamic_index_in_dim(chunks, 1 - core, axis=1, keepdims=False)
    summed_a = keep_a + swap_pairs(send_a.astype(jnp.bfloat16), 1).astype(jnp.float32)
    keep_b = lax.dynamic_index_in_dim(summed_a, chip, axis=0, keepdims=False)
    send_b = lax.dynamic_index_in_dim(summed_a, 1 - chip, axis=0, keepdims=False)
    mine = keep_b + swap_pairs(send_b.astype(jnp.bfloat16), 2).astype(jnp.float32)

    q_rows = block_len * q_width // HEAD_DIM
    q_mine = mine[:q_rows].reshape(block_len, q_width)
    k_mine = mine[q_rows : q_rows + key_len]
    v_mine = mine[q_rows + key_len :]

    block_start = seq_at * block_len
    q_pos = block_start + jnp.arange(block_len, dtype=jnp.int32)
    k_offset = core * key_len + jnp.arange(key_len, dtype=jnp.int32)
    query = rotate(q_mine, q_pos).astype(jnp.bfloat16)
    keys = rotate(k_mine, block_start + k_offset).astype(jnp.bfloat16)
    kv_own = jnp.concatenate([keys, v_mine.astype(jnp.bfloat16)], axis=1)

    query_other = swap_pairs(query, 1)
    q_all = jnp.concatenate([query, query_other], axis=1)
    q_heads = q_all.reshape(block_len, -1, HEAD_DIM).transpose(1, 0, 2)
    n_heads = q_heads.shape[0]

    def attend(state, kv_rows, allowed):
        peak, total, summed = state
        key_blk = kv_rows[:, :HEAD_DIM]
        value_blk = kv_rows[:, HEAD_DIM:]
        scores = (
            jnp.einsum("hqd,kd->hqk", q_heads, key_blk, preferred_element_type=jnp.float32)
            * score_scale
        )
        scores = jnp.where(allowed[None], scores, masked_score)
        new_peak = jnp.maximum(peak, jnp.max(scores, axis=-1))
        weights = jnp.exp(scores - new_peak[..., None])
        factor = jnp.exp(peak - new_peak)
        total = total * factor + jnp.sum(weights, axis=-1)
        summed = summed * factor[..., None] + jnp.einsum(
            "hqk,kd->hqd",
            weights.astype(jnp.bfloat16),
            value_blk,
            preferred_element_type=jnp.float32,
        )
        return (new_peak, total, summed)

    state = (
        jnp.full((n_heads, block_len), masked_score, jnp.float32),
        jnp.zeros((n_heads, block_len), jnp.float32),
        jnp.zeros((n_heads, block_len, HEAD_DIM), jnp.float32),
    )
    half = seq_count // 2
    z_at = seq_at % half
    base = seq_at - z_at
    z_fwd = [(s, s - s % half + (s + 1) % half) for s in range(seq_count)]
    z_bwd = [(s, s - s % half + (s - 1) % half) for s in range(seq_count)]
    across = [(s, (s + half) % seq_count) for s in range(seq_count)]
    steps = half // 2
    pending = [(kv_own, seq_at)]
    kv_fwd = kv_own
    kv_bwd = kv_own
    for step in range(1, steps + 2):
        arrived = []
        if step <= steps:
            kv_fwd = lax.ppermute(kv_fwd, "seq", z_fwd)
            arrived.append((kv_fwd, base + (z_at - step) % half))
            if step < steps:
                kv_bwd = lax.ppermute(kv_bwd, "seq", z_bwd)
                arrived.append((kv_bwd, base + (z_at + step) % half))
        got = lax.ppermute(jnp.stack([kv for kv, _ in pending]), "seq", across)
        crossed = [(got[i], (block + half) % seq_count) for i, (_, block) in enumerate(pending)]
        incoming = arrived + crossed
        if step == 1:
            incoming = incoming + [(kv_own, seq_at)]
        arrays, state = lax.optimization_barrier(([kv for kv, _ in incoming], state))
        kv_step = jnp.concatenate(arrays, axis=0)
        step_pos = jnp.concatenate([block * block_len + k_offset for _, block in incoming])
        state = attend(state, kv_step, step_pos[None, :] <= q_pos[:, None])
        pending = arrived

    peak, total, summed = state
    other_peak, other_total, other_norm = swap_pairs(
        (peak, total, (summed / total[..., None]).astype(jnp.bfloat16)), 1
    )
    other_peak, other_total, other_norm = (
        jnp.roll(part, n_heads // 2, axis=0) for part in (other_peak, other_total, other_norm)
    )
    peak_all = jnp.maximum(peak, other_peak)
    factor_a = jnp.exp(peak - peak_all)
    factor_b = jnp.exp(other_peak - peak_all) * other_total
    total_all = total * factor_a + factor_b
    summed_all = summed * factor_a[..., None] + other_norm.astype(jnp.float32) * factor_b[..., None]
    heads_all = (summed_all / total_all[..., None]).astype(jnp.bfloat16)
    own = n_heads // 2
    heads_pair = pick(
        core == 0,
        heads_all,
        jnp.concatenate([heads_all[own:], heads_all[:own]], axis=0),
    )
    heads_pair = heads_pair.reshape(2, own, block_len, HEAD_DIM).transpose(0, 2, 1, 3)
    heads_pair = heads_pair.reshape(2, block_len, q_width)
    got_x = swap_pairs(lax.dynamic_index_in_dim(heads_pair, core, 0, keepdims=False), 2)
    got_partner = swap_pairs(got_x, 1)
    heads_quad_other = jnp.stack(
        [pick(core == 0, got_x, got_partner), pick(core == 0, got_partner, got_x)]
    )
    heads_quad = jnp.concatenate(
        [pick(chip == 0, heads_pair, heads_quad_other), pick(chip == 0, heads_quad_other, heads_pair)]
    )
    w_out = w_output.reshape(row_count, q_width, w_output.shape[1])
    partial_out = jnp.einsum(
        "rtc,rco->to", heads_quad, w_out, preferred_element_type=jnp.float32
    ).astype(jnp.bfloat16)
    out_chunks = partial_out.reshape(col_count, shard_rows, -1)
    result = lax.dynamic_index_in_dim(out_chunks, col_at, 0, keepdims=False).astype(jnp.float32)
    for step in range(1, col_count):
        target = (col_at + step) % col_count
        sent = lax.dynamic_index_in_dim(out_chunks, target, 0, keepdims=False)
        result = result + shifted(sent, "col", step).astype(jnp.float32)
    return result.astype(jnp.bfloat16)


def solution(mesh):
    return jax.shard_map(
        on_device,
        mesh=mesh,
        in_specs=(
            P(("seq", "col"), "row"),
            P("row", "col"),
            P("row", "col"),
            P("row", "col"),
            P("col", "row"),
        ),
        out_specs=P(("seq", "col"), "row"),
        check_vma=False,
    )
```

```python
import jax
import jax.numpy as jnp
from jax import lax
from jax.sharding import PartitionSpec as P

HEADS = 32
KV_HEADS = 8
HEAD_DIM = 128


rope_base = 500000.0
masked_score = -1e30


def rotation_table(positions):
    half = HEAD_DIM // 2
    freqs = rope_base ** (-(jnp.arange(half, dtype=jnp.float32) * 2.0) / HEAD_DIM)
    angles = positions.astype(jnp.float32)[:, None] * freqs[None, :]
    cosine = jnp.concatenate([jnp.cos(angles), jnp.cos(angles)], axis=1)
    sine = jnp.concatenate([jnp.sin(angles), jnp.sin(angles)], axis=1)
    return cosine, sine


def rotate(values, table):
    half = HEAD_DIM // 2
    cosine, sine = table
    count = values.shape[0]
    heads = values.reshape(count, -1, HEAD_DIM)
    turned = jnp.concatenate([-heads[..., half:], heads[..., :half]], axis=-1)
    result = heads * cosine[:, None, :] + turned * sine[:, None, :]
    return result.reshape(count, -1)


def swap_pairs(value, flip):
    count = lax.axis_size("row")
    return lax.ppermute(value, "row", [(r, r ^ flip) for r in range(count)])


def shifted(value, axis, step):
    count = lax.axis_size(axis)
    return lax.ppermute(value, axis, [(i, (i + step) % count) for i in range(count)])


def pick(flag, first, second):
    return jnp.where(flag, first, second)


def on_device(tokens, w_query, w_key, w_value, w_output):
    shard_rows = tokens.shape[0]
    col_count = lax.axis_size("col")
    row_count = lax.axis_size("row")
    seq_count = lax.axis_size("seq")
    block_len = shard_rows * col_count
    key_len = block_len // 2
    seq_at = lax.axis_index("seq")
    row_at = lax.axis_index("row")
    core = row_at % 2
    chip = row_at // 2
    width_q = w_query.shape[1]
    width_kv = w_key.shape[1]
    local_kv = width_kv // HEAD_DIM
    assert row_count == 2 * local_kv
    q_width = width_q // row_count
    score_scale = HEAD_DIM ** (-0.5)

    col_at = lax.axis_index("col")
    pieces = [tokens] + [shifted(tokens, "col", step) for step in range(1, col_count)]
    order = (col_at - jnp.arange(col_count, dtype=jnp.int32)) % col_count
    block_tokens = jnp.take(jnp.stack(pieces), order, axis=0).reshape(block_len, -1)
    part_q = jnp.dot(block_tokens, w_query, preferred_element_type=jnp.float32)
    part_k = jnp.dot(block_tokens, w_key, preferred_element_type=jnp.float32)
    part_v = jnp.dot(block_tokens, w_value, preferred_element_type=jnp.float32)
    q_chunks = part_q.reshape(block_len, row_count, q_width).transpose(1, 0, 2)
    q_chunks = q_chunks.reshape(2, 2, block_len * q_width // HEAD_DIM, HEAD_DIM)

    def kv_chunks(part):
        split = part.reshape(2, key_len, local_kv, HEAD_DIM).transpose(2, 0, 1, 3)
        return split

    chunks = jnp.concatenate([q_chunks, kv_chunks(part_k), kv_chunks(part_v)], axis=2)
    keep_a = lax.dynamic_index_in_dim(chunks, core, axis=1, keepdims=False)
    send_a = lax.dynamic_index_in_dim(chunks, 1 - core, axis=1, keepdims=False)
    summed_a = keep_a + swap_pairs(send_a.astype(jnp.bfloat16), 1).astype(jnp.float32)
    keep_b = lax.dynamic_index_in_dim(summed_a, chip, axis=0, keepdims=False)
    send_b = lax.dynamic_index_in_dim(summed_a, 1 - chip, axis=0, keepdims=False)
    mine = keep_b + swap_pairs(send_b.astype(jnp.bfloat16), 2).astype(jnp.float32)

    q_rows = block_len * q_width // HEAD_DIM
    q_mine = mine[:q_rows].reshape(block_len, q_width)
    k_mine = mine[q_rows : q_rows + key_len]
    v_mine = mine[q_rows + key_len :]

    block_start = seq_at * block_len
    q_pos = block_start + jnp.arange(block_len, dtype=jnp.int32)
    k_offset = core * key_len + jnp.arange(key_len, dtype=jnp.int32)
    q_table = rotation_table(q_pos)
    k_table = tuple(
        lax.dynamic_slice_in_dim(part, core * key_len, key_len, 0) for part in q_table
    )
    query = rotate(q_mine, q_table).astype(jnp.bfloat16)
    keys = rotate(k_mine, k_table).astype(jnp.bfloat16)
    kv_own = jnp.concatenate([keys, v_mine.astype(jnp.bfloat16)], axis=1)

    query_other = swap_pairs(query, 1)
    q_all = jnp.concatenate([query, query_other], axis=1)
    q_heads = q_all.reshape(block_len, -1, HEAD_DIM).transpose(1, 0, 2)
    n_heads = q_heads.shape[0]

    def attend(state, kv_rows, allowed):
        peak, total, summed = state
        key_blk = kv_rows[:, :HEAD_DIM]
        value_blk = kv_rows[:, HEAD_DIM:]
        scores = (
            jnp.einsum("hqd,kd->hqk", q_heads, key_blk, preferred_element_type=jnp.float32)
            * score_scale
        )
        scores = jnp.where(allowed[None], scores, masked_score)
        new_peak = jnp.maximum(peak, jnp.max(scores, axis=-1))
        weights = jnp.exp(scores - new_peak[..., None])
        factor = jnp.exp(peak - new_peak)
        total = total * factor + jnp.sum(weights, axis=-1)
        summed = summed * factor[..., None] + jnp.einsum(
            "hqk,kd->hqd",
            weights.astype(jnp.bfloat16),
            value_blk,
            preferred_element_type=jnp.float32,
        )
        return (new_peak, total, summed)

    state = (
        jnp.full((n_heads, block_len), masked_score, jnp.float32),
        jnp.zeros((n_heads, block_len), jnp.float32),
        jnp.zeros((n_heads, block_len, HEAD_DIM), jnp.float32),
    )
    own_pos = block_start + k_offset
    state = attend(state, kv_own, own_pos[None, :] <= q_pos[:, None])
    half = seq_count // 2
    z_at = seq_at % half
    base = seq_at - z_at
    z_fwd = [(s, s - s % half + (s + 1) % half) for s in range(seq_count)]
    z_bwd = [(s, s - s % half + (s - 1) % half) for s in range(seq_count)]
    across = [(s, (s + half) % seq_count) for s in range(seq_count)]
    steps = half // 2
    pending = [(kv_own, seq_at)]
    kv_fwd = kv_own
    kv_bwd = kv_own
    for step in range(1, steps + 2):
        arrived = []
        if step <= steps:
            kv_fwd = lax.ppermute(kv_fwd, "seq", z_fwd)
            arrived.append((kv_fwd, base + (z_at - step) % half))
            if step < steps:
                kv_bwd = lax.ppermute(kv_bwd, "seq", z_bwd)
                arrived.append((kv_bwd, base + (z_at + step) % half))
        got = lax.ppermute(jnp.stack([kv for kv, _ in pending]), "seq", across)
        crossed = [(got[i], (block + half) % seq_count) for i, (_, block) in enumerate(pending)]
        incoming = arrived + crossed
        arrays, state = lax.optimization_barrier(([kv for kv, _ in incoming], state))
        kv_step = jnp.concatenate(arrays, axis=0)
        step_pos = jnp.concatenate([block * block_len + k_offset for _, block in incoming])
        state = attend(state, kv_step, (step_pos < block_start)[None, :])
        pending = arrived

    peak, total, summed = state
    other_peak, other_total, other_norm = swap_pairs(
        (peak, total, (summed / total[..., None]).astype(jnp.bfloat16)), 1
    )
    other_peak, other_total, other_norm = (
        jnp.roll(part, n_heads // 2, axis=0) for part in (other_peak, other_total, other_norm)
    )
    peak_all = jnp.maximum(peak, other_peak)
    factor_a = jnp.exp(peak - peak_all)
    factor_b = jnp.exp(other_peak - peak_all) * other_total
    total_all = total * factor_a + factor_b
    summed_all = summed * factor_a[..., None] + other_norm.astype(jnp.float32) * factor_b[..., None]
    heads_all = (summed_all / total_all[..., None]).astype(jnp.bfloat16)
    own = n_heads // 2
    heads_pair = pick(
        core == 0,
        heads_all,
        jnp.concatenate([heads_all[own:], heads_all[:own]], axis=0),
    )
    heads_pair = heads_pair.reshape(2, own, block_len, HEAD_DIM).transpose(0, 2, 1, 3)
    heads_pair = heads_pair.reshape(2, block_len, q_width)
    got_x = swap_pairs(lax.dynamic_index_in_dim(heads_pair, core, 0, keepdims=False), 2)
    got_partner = swap_pairs(got_x, 1)
    heads_quad_other = jnp.stack(
        [pick(core == 0, got_x, got_partner), pick(core == 0, got_partner, got_x)]
    )
    heads_quad = jnp.concatenate(
        [pick(chip == 0, heads_pair, heads_quad_other), pick(chip == 0, heads_quad_other, heads_pair)]
    )
    w_out = w_output.reshape(row_count, q_width, w_output.shape[1])
    partial_out = jnp.einsum(
        "rtc,rco->to", heads_quad, w_out, preferred_element_type=jnp.float32
    ).astype(jnp.bfloat16)
    out_chunks = partial_out.reshape(col_count, shard_rows, -1)
    result = lax.dynamic_index_in_dim(out_chunks, col_at, 0, keepdims=False).astype(jnp.float32)
    for step in range(1, col_count):
        target = (col_at + step) % col_count
        sent = lax.dynamic_index_in_dim(out_chunks, target, 0, keepdims=False)
        result = result + shifted(sent, "col", step).astype(jnp.float32)
    return result.astype(jnp.bfloat16)


def solution(mesh):
    return jax.shard_map(
        on_device,
        mesh=mesh,
        in_specs=(
            P(("seq", "col"), "row"),
            P("row", "col"),
            P("row", "col"),
            P("row", "col"),
            P("col", "row"),
        ),
        out_specs=P(("seq", "col"), "row"),
        check_vma=False,
    )
```

```python
import jax
import jax.numpy as jnp
from jax import lax
from jax.sharding import PartitionSpec as P

HEADS = 32
KV_HEADS = 8
HEAD_DIM = 128


rope_base = 500000.0
masked_score = -1e30


def rotation_table(positions):
    half = HEAD_DIM // 2
    freqs = rope_base ** (-(jnp.arange(half, dtype=jnp.float32) * 2.0) / HEAD_DIM)
    angles = positions.astype(jnp.float32)[:, None] * freqs[None, :]
    cosine = jnp.concatenate([jnp.cos(angles), jnp.cos(angles)], axis=1)
    sine = jnp.concatenate([jnp.sin(angles), jnp.sin(angles)], axis=1)
    return cosine, sine


def rotate(values, table):
    half = HEAD_DIM // 2
    cosine, sine = table
    count = values.shape[0]
    heads = values.reshape(count, -1, HEAD_DIM)
    turned = jnp.concatenate([-heads[..., half:], heads[..., :half]], axis=-1)
    result = heads * cosine[:, None, :] + turned * sine[:, None, :]
    return result.reshape(count, -1)


def swap_pairs(value, flip):
    count = lax.axis_size("row")
    return lax.ppermute(value, "row", [(r, r ^ flip) for r in range(count)])


def shifted(value, axis, step):
    count = lax.axis_size(axis)
    return lax.ppermute(value, axis, [(i, (i + step) % count) for i in range(count)])


def pick(flag, first, second):
    return jnp.where(flag, first, second)


def on_device(tokens, w_query, w_key, w_value, w_output):
    shard_rows = tokens.shape[0]
    col_count = lax.axis_size("col")
    row_count = lax.axis_size("row")
    seq_count = lax.axis_size("seq")
    block_len = shard_rows * col_count
    key_len = block_len // 2
    seq_at = lax.axis_index("seq")
    row_at = lax.axis_index("row")
    core = row_at % 2
    chip = row_at // 2
    width_q = w_query.shape[1]
    width_kv = w_key.shape[1]
    local_kv = width_kv // HEAD_DIM
    assert row_count == 2 * local_kv
    q_width = width_q // row_count
    score_scale = HEAD_DIM ** (-0.5)

    col_at = lax.axis_index("col")
    pieces = [tokens] + [shifted(tokens, "col", step) for step in range(1, col_count)]
    order = (col_at - jnp.arange(col_count, dtype=jnp.int32)) % col_count
    block_tokens = jnp.take(jnp.stack(pieces), order, axis=0).reshape(block_len, -1)
    part_q = jnp.dot(block_tokens, w_query, preferred_element_type=jnp.float32)
    part_k = jnp.dot(block_tokens, w_key, preferred_element_type=jnp.float32)
    part_v = jnp.dot(block_tokens, w_value, preferred_element_type=jnp.float32)
    q_chunks = part_q.reshape(block_len, row_count, q_width).transpose(1, 0, 2)
    q_chunks = q_chunks.reshape(2, 2, block_len * q_width // HEAD_DIM, HEAD_DIM)

    def kv_chunks(part):
        split = part.reshape(2, key_len, local_kv, HEAD_DIM).transpose(2, 0, 1, 3)
        return split

    chunks = jnp.concatenate([q_chunks, kv_chunks(part_k), kv_chunks(part_v)], axis=2)
    keep_a = lax.dynamic_index_in_dim(chunks, core, axis=1, keepdims=False)
    send_a = lax.dynamic_index_in_dim(chunks, 1 - core, axis=1, keepdims=False)
    summed_a = keep_a + swap_pairs(send_a.astype(jnp.bfloat16), 1).astype(jnp.float32)
    keep_b = lax.dynamic_index_in_dim(summed_a, chip, axis=0, keepdims=False)
    send_b = lax.dynamic_index_in_dim(summed_a, 1 - chip, axis=0, keepdims=False)
    mine = keep_b + swap_pairs(send_b.astype(jnp.bfloat16), 2).astype(jnp.float32)

    q_rows = block_len * q_width // HEAD_DIM
    q_mine = mine[:q_rows].reshape(block_len, q_width)
    k_mine = mine[q_rows : q_rows + key_len]
    v_mine = mine[q_rows + key_len :]

    block_start = seq_at * block_len
    q_pos = block_start + jnp.arange(block_len, dtype=jnp.int32)
    k_offset = core * key_len + jnp.arange(key_len, dtype=jnp.int32)
    q_table = rotation_table(q_pos)
    k_table = tuple(
        lax.dynamic_slice_in_dim(part, core * key_len, key_len, 0) for part in q_table
    )
    query = rotate(q_mine, q_table).astype(jnp.bfloat16)
    keys = rotate(k_mine, k_table).astype(jnp.bfloat16)
    kv_own = jnp.concatenate([keys, v_mine.astype(jnp.bfloat16)], axis=1)

    query_other = swap_pairs(query, 1)
    q_all = jnp.concatenate([query, query_other], axis=1)
    q_heads = q_all.reshape(block_len, -1, HEAD_DIM).transpose(1, 0, 2)
    n_heads = q_heads.shape[0]

    def attend(state, kv_rows, allowed):
        peak, total, summed = state
        key_blk = kv_rows[:, :HEAD_DIM]
        value_blk = kv_rows[:, HEAD_DIM:]
        scores = (
            jnp.einsum("hqd,kd->hqk", q_heads, key_blk, preferred_element_type=jnp.float32)
            * score_scale
        )
        scores = jnp.where(allowed[None], scores, masked_score)
        new_peak = jnp.maximum(peak, jnp.max(scores, axis=-1))
        weights = jnp.exp(scores - new_peak[..., None])
        factor = jnp.exp(peak - new_peak)
        total = total * factor + jnp.sum(weights, axis=-1)
        summed = summed * factor[..., None] + jnp.einsum(
            "hqk,kd->hqd",
            weights.astype(jnp.bfloat16),
            value_blk,
            preferred_element_type=jnp.float32,
        )
        return (new_peak, total, summed)

    state = (
        jnp.full((n_heads, block_len), masked_score, jnp.float32),
        jnp.zeros((n_heads, block_len), jnp.float32),
        jnp.zeros((n_heads, block_len, HEAD_DIM), jnp.float32),
    )
    half = seq_count // 2
    z_at = seq_at % half
    base = seq_at - z_at
    z_fwd = [(s, s - s % half + (s + 1) % half) for s in range(seq_count)]
    z_bwd = [(s, s - s % half + (s - 1) % half) for s in range(seq_count)]
    across = [(s, (s + half) % seq_count) for s in range(seq_count)]
    steps = half // 2
    pending = [(kv_own, seq_at)]
    kv_fwd = kv_own
    kv_bwd = kv_own
    for step in range(1, steps + 2):
        arrived = []
        if step <= steps:
            kv_fwd = lax.ppermute(kv_fwd, "seq", z_fwd)
            arrived.append((kv_fwd, base + (z_at - step) % half))
            if step < steps:
                kv_bwd = lax.ppermute(kv_bwd, "seq", z_bwd)
                arrived.append((kv_bwd, base + (z_at + step) % half))
        got = lax.ppermute(jnp.stack([kv for kv, _ in pending]), "seq", across)
        crossed = [(got[i], (block + half) % seq_count) for i, (_, block) in enumerate(pending)]
        incoming = arrived + crossed
        arrays, state = lax.optimization_barrier(([kv for kv, _ in incoming], state))
        kv_step = jnp.concatenate(arrays, axis=0)
        step_pos = jnp.concatenate([block * block_len + k_offset for _, block in incoming])
        state = attend(state, kv_step, (step_pos < block_start)[None, :])
        pending = arrived

    own_pos = block_start + k_offset
    state = attend(state, kv_own, own_pos[None, :] <= q_pos[:, None])

    peak, total, summed = state
    other_peak, other_total, other_norm = swap_pairs(
        (peak, total, (summed / total[..., None]).astype(jnp.bfloat16)), 1
    )
    other_peak, other_total, other_norm = (
        jnp.roll(part, n_heads // 2, axis=0) for part in (other_peak, other_total, other_norm)
    )
    peak_all = jnp.maximum(peak, other_peak)
    factor_a = jnp.exp(peak - peak_all)
    factor_b = jnp.exp(other_peak - peak_all) * other_total
    total_all = total * factor_a + factor_b
    summed_all = summed * factor_a[..., None] + other_norm.astype(jnp.float32) * factor_b[..., None]
    heads_all = (summed_all / total_all[..., None]).astype(jnp.bfloat16)
    own = n_heads // 2
    heads_pair = pick(
        core == 0,
        heads_all,
        jnp.concatenate([heads_all[own:], heads_all[:own]], axis=0),
    )
    heads_pair = heads_pair.reshape(2, own, block_len, HEAD_DIM).transpose(0, 2, 1, 3)
    heads_pair = heads_pair.reshape(2, block_len, q_width)
    got_x = swap_pairs(lax.dynamic_index_in_dim(heads_pair, core, 0, keepdims=False), 2)
    got_partner = swap_pairs(got_x, 1)
    heads_quad_other = jnp.stack(
        [pick(core == 0, got_x, got_partner), pick(core == 0, got_partner, got_x)]
    )
    heads_quad = jnp.concatenate(
        [pick(chip == 0, heads_pair, heads_quad_other), pick(chip == 0, heads_quad_other, heads_pair)]
    )
    w_out = w_output.reshape(row_count, q_width, w_output.shape[1])
    partial_out = jnp.einsum(
        "rtc,rco->to", heads_quad, w_out, preferred_element_type=jnp.float32
    ).astype(jnp.bfloat16)
    out_chunks = partial_out.reshape(col_count, shard_rows, -1)
    result = lax.dynamic_index_in_dim(out_chunks, col_at, 0, keepdims=False).astype(jnp.float32)
    for step in range(1, col_count):
        target = (col_at + step) % col_count
        sent = lax.dynamic_index_in_dim(out_chunks, target, 0, keepdims=False)
        result = result + shifted(sent, "col", step).astype(jnp.float32)
    return result.astype(jnp.bfloat16)


def solution(mesh):
    return jax.shard_map(
        on_device,
        mesh=mesh,
        in_specs=(
            P(("seq", "col"), "row"),
            P("row", "col"),
            P("row", "col"),
            P("row", "col"),
            P("col", "row"),
        ),
        out_specs=P(("seq", "col"), "row"),
        check_vma=False,
    )
```

```python
import jax
import jax.numpy as jnp
from jax import lax
from jax.sharding import PartitionSpec as P

HEADS = 32
KV_HEADS = 8
HEAD_DIM = 128


rope_base = 500000.0
masked_score = -1e30


def rotation_table(positions):
    half = HEAD_DIM // 2
    freqs = rope_base ** (-(jnp.arange(half, dtype=jnp.float32) * 2.0) / HEAD_DIM)
    angles = positions.astype(jnp.float32)[:, None] * freqs[None, :]
    cosine = jnp.concatenate([jnp.cos(angles), jnp.cos(angles)], axis=1)
    sine = jnp.concatenate([jnp.sin(angles), jnp.sin(angles)], axis=1)
    return cosine, sine


def rotate(values, table):
    half = HEAD_DIM // 2
    cosine, sine = table
    count = values.shape[0]
    heads = values.reshape(count, -1, HEAD_DIM)
    turned = jnp.concatenate([-heads[..., half:], heads[..., :half]], axis=-1)
    result = heads * cosine[:, None, :] + turned * sine[:, None, :]
    return result.reshape(count, -1)


def swap_pairs(value, flip):
    count = lax.axis_size("row")
    return lax.ppermute(value, "row", [(r, r ^ flip) for r in range(count)])


def shifted(value, axis, step):
    count = lax.axis_size(axis)
    return lax.ppermute(value, axis, [(i, (i + step) % count) for i in range(count)])


def pick(flag, first, second):
    return jnp.where(flag, first, second)


def on_device(tokens, w_query, w_key, w_value, w_output):
    shard_rows = tokens.shape[0]
    col_count = lax.axis_size("col")
    row_count = lax.axis_size("row")
    seq_count = lax.axis_size("seq")
    block_len = shard_rows * col_count
    key_len = block_len // 2
    seq_at = lax.axis_index("seq")
    row_at = lax.axis_index("row")
    core = row_at % 2
    chip = row_at // 2
    width_q = w_query.shape[1]
    width_kv = w_key.shape[1]
    local_kv = width_kv // HEAD_DIM
    assert row_count == 2 * local_kv
    q_width = width_q // row_count
    score_scale = HEAD_DIM ** (-0.5)

    col_at = lax.axis_index("col")
    pieces = [tokens] + [shifted(tokens, "col", step) for step in range(1, col_count)]
    order = (col_at - jnp.arange(col_count, dtype=jnp.int32)) % col_count
    block_tokens = jnp.take(jnp.stack(pieces), order, axis=0).reshape(block_len, -1)
    part_q = jnp.dot(block_tokens, w_query, preferred_element_type=jnp.float32)
    part_k = jnp.dot(block_tokens, w_key, preferred_element_type=jnp.float32)
    part_v = jnp.dot(block_tokens, w_value, preferred_element_type=jnp.float32)
    q_chunks = part_q.reshape(block_len, row_count, q_width).transpose(1, 0, 2)
    q_chunks = q_chunks.reshape(2, 2, block_len * q_width // HEAD_DIM, HEAD_DIM)

    def kv_chunks(part):
        split = part.reshape(2, key_len, local_kv, HEAD_DIM).transpose(2, 0, 1, 3)
        return split

    chunks = jnp.concatenate([q_chunks, kv_chunks(part_k), kv_chunks(part_v)], axis=2)
    keep_a = lax.dynamic_index_in_dim(chunks, core, axis=1, keepdims=False)
    send_a = lax.dynamic_index_in_dim(chunks, 1 - core, axis=1, keepdims=False)
    summed_a = keep_a + swap_pairs(send_a.astype(jnp.bfloat16), 1).astype(jnp.float32)
    keep_b = lax.dynamic_index_in_dim(summed_a, chip, axis=0, keepdims=False)
    send_b = lax.dynamic_index_in_dim(summed_a, 1 - chip, axis=0, keepdims=False)
    mine = keep_b + swap_pairs(send_b.astype(jnp.bfloat16), 2).astype(jnp.float32)

    q_rows = block_len * q_width // HEAD_DIM
    q_mine = mine[:q_rows].reshape(block_len, q_width)
    k_mine = mine[q_rows : q_rows + key_len]
    v_mine = mine[q_rows + key_len :]

    block_start = seq_at * block_len
    q_pos = block_start + jnp.arange(block_len, dtype=jnp.int32)
    k_offset = core * key_len + jnp.arange(key_len, dtype=jnp.int32)
    q_table = rotation_table(q_pos)
    k_table = tuple(
        lax.dynamic_slice_in_dim(part, core * key_len, key_len, 0) for part in q_table
    )
    query = rotate(q_mine, q_table).astype(jnp.bfloat16)
    keys = rotate(k_mine, k_table).astype(jnp.bfloat16)
    kv_own = jnp.concatenate([keys, v_mine.astype(jnp.bfloat16)], axis=1)

    query_other = swap_pairs(query, 1)
    q_all = jnp.concatenate([query, query_other], axis=1)
    q_heads = q_all.reshape(block_len, -1, HEAD_DIM).transpose(1, 0, 2)
    n_heads = q_heads.shape[0]

    def attend(state, kv_rows, allowed):
        peak, total, summed = state
        key_blk = kv_rows[:, :HEAD_DIM]
        value_blk = kv_rows[:, HEAD_DIM:]
        scores = (
            jnp.einsum("hqd,kd->hqk", q_heads, key_blk, preferred_element_type=jnp.float32)
            * score_scale
        )
        scores = jnp.where(allowed[None], scores, masked_score)
        new_peak = jnp.maximum(peak, jnp.max(scores, axis=-1))
        weights = jnp.exp(scores - new_peak[..., None])
        factor = jnp.exp(peak - new_peak)
        total = total * factor + jnp.sum(weights, axis=-1)
        summed = summed * factor[..., None] + jnp.einsum(
            "hqk,kd->hqd",
            weights.astype(jnp.bfloat16),
            value_blk,
            preferred_element_type=jnp.float32,
        )
        return (new_peak, total, summed)

    state = (
        jnp.full((n_heads, block_len), masked_score, jnp.float32),
        jnp.zeros((n_heads, block_len), jnp.float32),
        jnp.zeros((n_heads, block_len, HEAD_DIM), jnp.float32),
    )
    half = seq_count // 2
    z_at = seq_at % half
    base = seq_at - z_at
    z_fwd = [(s, s - s % half + (s + 1) % half) for s in range(seq_count)]
    z_bwd = [(s, s - s % half + (s - 1) % half) for s in range(seq_count)]
    across = [(s, (s + half) % seq_count) for s in range(seq_count)]
    steps = half // 2
    pending = [(kv_own, seq_at)]
    kv_fwd = kv_own
    kv_bwd = kv_own
    for step in range(1, steps + 2):
        arrived = []
        if step <= steps:
            kv_fwd = lax.ppermute(kv_fwd, "seq", z_fwd)
            arrived.append((kv_fwd, base + (z_at - step) % half))
            if step < steps:
                kv_bwd = lax.ppermute(kv_bwd, "seq", z_bwd)
                arrived.append((kv_bwd, base + (z_at + step) % half))
        got = lax.ppermute(jnp.stack([kv for kv, _ in pending]), "seq", across)
        crossed = [(got[i], (block + half) % seq_count) for i, (_, block) in enumerate(pending)]
        incoming = arrived + crossed
        arrays, state = lax.optimization_barrier(([kv for kv, _ in incoming], state))
        kv_step = jnp.concatenate(arrays, axis=0)
        step_pos = jnp.concatenate([block * block_len + k_offset for _, block in incoming])
        state = attend(state, kv_step, (step_pos < block_start)[None, :])
        pending = arrived

    own_pos = block_start + k_offset
    state = attend(state, kv_own, own_pos[None, :] <= q_pos[:, None])

    peak, total, summed = state
    other_peak, other_total, other_norm = swap_pairs(
        (peak, total, (summed / total[..., None]).astype(jnp.bfloat16)), 1
    )
    other_peak, other_total, other_norm = (
        jnp.roll(part, n_heads // 2, axis=0) for part in (other_peak, other_total, other_norm)
    )
    peak_all = jnp.maximum(peak, other_peak)
    factor_a = jnp.exp(peak - peak_all)
    factor_b = jnp.exp(other_peak - peak_all) * other_total
    total_all = total * factor_a + factor_b
    summed_all = summed * factor_a[..., None] + other_norm.astype(jnp.float32) * factor_b[..., None]
    heads_all = (summed_all / total_all[..., None]).astype(jnp.bfloat16)
    own = n_heads // 2
    heads_pair = pick(
        core == 0,
        heads_all,
        jnp.concatenate([heads_all[own:], heads_all[:own]], axis=0),
    )
    heads_pair = heads_pair.reshape(2, own, block_len, HEAD_DIM).transpose(0, 2, 1, 3)
    heads_pair = heads_pair.reshape(2, block_len, q_width)
    got_x = swap_pairs(lax.dynamic_index_in_dim(heads_pair, core, 0, keepdims=False), 2)
    got_partner = swap_pairs(got_x, 1)
    heads_quad_other = jnp.stack(
        [pick(core == 0, got_x, got_partner), pick(core == 0, got_partner, got_x)]
    )
    w_out = w_output.reshape(row_count, q_width, w_output.shape[1])
    w_local = lax.dynamic_slice_in_dim(w_out, 2 * chip, 2, 0)
    w_remote = lax.dynamic_slice_in_dim(w_out, 2 * (1 - chip), 2, 0)
    partial_local = jnp.einsum("rtc,rco->to", heads_pair, w_local, preferred_element_type=jnp.float32)
    partial_remote = jnp.einsum(
        "rtc,rco->to", heads_quad_other, w_remote, preferred_element_type=jnp.float32
    )
    partial_out = (partial_local + partial_remote).astype(jnp.bfloat16)
    out_chunks = partial_out.reshape(col_count, shard_rows, -1)
    result = lax.dynamic_index_in_dim(out_chunks, col_at, 0, keepdims=False).astype(jnp.float32)
    for step in range(1, col_count):
        target = (col_at + step) % col_count
        sent = lax.dynamic_index_in_dim(out_chunks, target, 0, keepdims=False)
        result = result + shifted(sent, "col", step).astype(jnp.float32)
    return result.astype(jnp.bfloat16)


def solution(mesh):
    return jax.shard_map(
        on_device,
        mesh=mesh,
        in_specs=(
            P(("seq", "col"), "row"),
            P("row", "col"),
            P("row", "col"),
            P("row", "col"),
            P("col", "row"),
        ),
        out_specs=P(("seq", "col"), "row"),
        check_vma=False,
    )
```

```python
import jax
import jax.numpy as jnp
from jax import lax
from jax.sharding import PartitionSpec as P

HEADS = 32
KV_HEADS = 8
HEAD_DIM = 128


rope_base = 500000.0
masked_score = -1e30


def rotation_table(positions):
    half = HEAD_DIM // 2
    freqs = rope_base ** (-(jnp.arange(half, dtype=jnp.float32) * 2.0) / HEAD_DIM)
    angles = positions.astype(jnp.float32)[:, None] * freqs[None, :]
    cosine = jnp.concatenate([jnp.cos(angles), jnp.cos(angles)], axis=1)
    sine = jnp.concatenate([jnp.sin(angles), jnp.sin(angles)], axis=1)
    return cosine, sine


def rotate(values, table):
    half = HEAD_DIM // 2
    cosine, sine = table
    count = values.shape[0]
    heads = values.reshape(count, -1, HEAD_DIM)
    turned = jnp.concatenate([-heads[..., half:], heads[..., :half]], axis=-1)
    result = heads * cosine[:, None, :] + turned * sine[:, None, :]
    return result.reshape(count, -1)


def swap_pairs(value, flip):
    count = lax.axis_size("row")
    return lax.ppermute(value, "row", [(r, r ^ flip) for r in range(count)])


def shifted(value, axis, step):
    count = lax.axis_size(axis)
    return lax.ppermute(value, axis, [(i, (i + step) % count) for i in range(count)])


def pick(flag, first, second):
    return jnp.where(flag, first, second)


def on_device(tokens, w_query, w_key, w_value, w_output):
    shard_rows = tokens.shape[0]
    col_count = lax.axis_size("col")
    row_count = lax.axis_size("row")
    seq_count = lax.axis_size("seq")
    block_len = shard_rows * col_count
    key_len = block_len // 2
    seq_at = lax.axis_index("seq")
    row_at = lax.axis_index("row")
    core = row_at % 2
    chip = row_at // 2
    width_q = w_query.shape[1]
    width_kv = w_key.shape[1]
    local_kv = width_kv // HEAD_DIM
    assert row_count == 2 * local_kv
    q_width = width_q // row_count
    score_scale = HEAD_DIM ** (-0.5)

    col_at = lax.axis_index("col")
    pieces = [tokens] + [shifted(tokens, "col", step) for step in range(1, col_count)]
    order = (col_at - jnp.arange(col_count, dtype=jnp.int32)) % col_count
    block_tokens = jnp.take(jnp.stack(pieces), order, axis=0).reshape(block_len, -1)
    part_q = jnp.dot(block_tokens, w_query, preferred_element_type=jnp.float32)
    part_k = jnp.dot(block_tokens, w_key, preferred_element_type=jnp.float32)
    part_v = jnp.dot(block_tokens, w_value, preferred_element_type=jnp.float32)
    q_chunks = part_q.reshape(block_len, row_count, q_width).transpose(1, 0, 2)
    q_chunks = q_chunks.reshape(2, 2, block_len * q_width // HEAD_DIM, HEAD_DIM)

    def kv_chunks(part):
        split = part.reshape(2, key_len, local_kv, HEAD_DIM).transpose(2, 0, 1, 3)
        return split

    chunks = jnp.concatenate([q_chunks, kv_chunks(part_k), kv_chunks(part_v)], axis=2)
    keep_a = lax.dynamic_index_in_dim(chunks, core, axis=1, keepdims=False)
    send_a = lax.dynamic_index_in_dim(chunks, 1 - core, axis=1, keepdims=False)
    summed_a = keep_a + swap_pairs(send_a.astype(jnp.bfloat16), 1).astype(jnp.float32)
    keep_b = lax.dynamic_index_in_dim(summed_a, chip, axis=0, keepdims=False)
    send_b = lax.dynamic_index_in_dim(summed_a, 1 - chip, axis=0, keepdims=False)
    mine = keep_b + swap_pairs(send_b.astype(jnp.bfloat16), 2).astype(jnp.float32)

    q_rows = block_len * q_width // HEAD_DIM
    q_mine = mine[:q_rows].reshape(block_len, q_width)
    k_mine = mine[q_rows : q_rows + key_len]
    v_mine = mine[q_rows + key_len :]

    block_start = seq_at * block_len
    q_pos = block_start + jnp.arange(block_len, dtype=jnp.int32)
    k_offset = core * key_len + jnp.arange(key_len, dtype=jnp.int32)
    q_table = rotation_table(q_pos)
    k_table = tuple(
        lax.dynamic_slice_in_dim(part, core * key_len, key_len, 0) for part in q_table
    )
    query = rotate(q_mine, q_table).astype(jnp.bfloat16)
    keys = rotate(k_mine, k_table).astype(jnp.bfloat16)
    kv_own = jnp.concatenate([keys, v_mine.astype(jnp.bfloat16)], axis=1)

    query_other = swap_pairs(query, 1)
    q_all = jnp.concatenate([query, query_other], axis=1)
    q_heads = q_all.reshape(block_len, -1, HEAD_DIM).transpose(1, 0, 2)
    n_heads = q_heads.shape[0]

    def attend(state, kv_rows, allowed):
        peak, total, summed = state
        key_blk = kv_rows[:, :HEAD_DIM]
        value_blk = kv_rows[:, HEAD_DIM:]
        scores = (
            jnp.einsum("hqd,kd->hqk", q_heads, key_blk, preferred_element_type=jnp.float32)
            * score_scale
        )
        scores = jnp.where(allowed[None], scores, masked_score)
        new_peak = jnp.maximum(peak, jnp.max(scores, axis=-1))
        weights = jnp.exp(scores - new_peak[..., None])
        factor = jnp.exp(peak - new_peak)
        total = total * factor + jnp.sum(weights, axis=-1)
        summed = summed * factor[..., None] + jnp.einsum(
            "hqk,kd->hqd",
            weights.astype(jnp.bfloat16),
            value_blk,
            preferred_element_type=jnp.float32,
        )
        return (new_peak, total, summed)

    state = (
        jnp.full((n_heads, block_len), masked_score, jnp.float32),
        jnp.zeros((n_heads, block_len), jnp.float32),
        jnp.zeros((n_heads, block_len, HEAD_DIM), jnp.float32),
    )
    half = seq_count // 2
    z_at = seq_at % half
    base = seq_at - z_at
    z_fwd = [(s, s - s % half + (s + 1) % half) for s in range(seq_count)]
    z_bwd = [(s, s - s % half + (s - 1) % half) for s in range(seq_count)]
    across = [(s, (s + half) % seq_count) for s in range(seq_count)]
    steps = half // 2
    pending = [(kv_own, seq_at)]
    kv_fwd = kv_own
    kv_bwd = kv_own
    for step in range(1, steps + 2):
        arrived = []
        if step <= steps:
            kv_fwd = lax.ppermute(kv_fwd, "seq", z_fwd)
            arrived.append((kv_fwd, base + (z_at - step) % half))
            if step < steps:
                kv_bwd = lax.ppermute(kv_bwd, "seq", z_bwd)
                arrived.append((kv_bwd, base + (z_at + step) % half))
        got = lax.ppermute(jnp.stack([kv for kv, _ in pending]), "seq", across)
        crossed = [(got[i], (block + half) % seq_count) for i, (_, block) in enumerate(pending)]
        incoming = arrived + crossed
        arrays, state = lax.optimization_barrier(([kv for kv, _ in incoming], state))
        kv_step = jnp.concatenate(arrays, axis=0)
        step_pos = jnp.concatenate([block * block_len + k_offset for _, block in incoming])
        state = attend(state, kv_step, (step_pos < block_start)[None, :])
        pending = arrived

    own_pos = block_start + k_offset
    state = attend(state, kv_own, own_pos[None, :] <= q_pos[:, None])

    peak, total, summed = state
    other_peak, other_total, other_norm = swap_pairs(
        (peak, total, (summed / total[..., None]).astype(jnp.bfloat16)), 1
    )
    other_peak, other_total, other_norm = (
        jnp.roll(part, n_heads // 2, axis=0) for part in (other_peak, other_total, other_norm)
    )
    peak_all = jnp.maximum(peak, other_peak)
    factor_a = jnp.exp(peak - peak_all)
    factor_b = jnp.exp(other_peak - peak_all) * other_total
    total_all = total * factor_a + factor_b
    summed_all = summed * factor_a[..., None] + other_norm.astype(jnp.float32) * factor_b[..., None]
    heads_all = (summed_all / total_all[..., None]).astype(jnp.bfloat16)
    own = n_heads // 2
    heads_pair = pick(
        core == 0,
        heads_all,
        jnp.concatenate([heads_all[own:], heads_all[:own]], axis=0),
    )
    heads_pair = heads_pair.reshape(2, own, block_len, HEAD_DIM).transpose(0, 2, 1, 3)
    heads_pair = heads_pair.reshape(2, block_len, q_width)
    got_x = swap_pairs(lax.dynamic_index_in_dim(heads_pair, core, 0, keepdims=False), 2)
    got_partner = swap_pairs(got_x, 1)
    heads_quad_other = jnp.stack(
        [pick(core == 0, got_x, got_partner), pick(core == 0, got_partner, got_x)]
    )
    w_out = w_output.reshape(row_count, q_width, w_output.shape[1])
    w_local = lax.dynamic_slice_in_dim(w_out, 2 * chip, 2, 0)
    w_remote = lax.dynamic_slice_in_dim(w_out, 2 * (1 - chip), 2, 0)
    def rows_for(col_index):
        start = col_index * shard_rows
        local = lax.dynamic_slice_in_dim(heads_pair, start, shard_rows, 1)
        remote = lax.dynamic_slice_in_dim(heads_quad_other, start, shard_rows, 1)
        part = jnp.einsum("rtc,rco->to", local, w_local, preferred_element_type=jnp.float32)
        part = part + jnp.einsum("rtc,rco->to", remote, w_remote, preferred_element_type=jnp.float32)
        return part.astype(jnp.bfloat16)

    received = []
    for step in range(1, col_count):
        received.append(shifted(rows_for((col_at + step) % col_count), "col", step))
    result = rows_for(col_at).astype(jnp.float32)
    for part in received:
        result = result + part.astype(jnp.float32)
    return result.astype(jnp.bfloat16)


def solution(mesh):
    return jax.shard_map(
        on_device,
        mesh=mesh,
        in_specs=(
            P(("seq", "col"), "row"),
            P("row", "col"),
            P("row", "col"),
            P("row", "col"),
            P("col", "row"),
        ),
        out_specs=P(("seq", "col"), "row"),
        check_vma=False,
    )
```

```python
import jax
import jax.numpy as jnp
from jax import lax
from jax.sharding import PartitionSpec as P

HEADS = 32
KV_HEADS = 8
HEAD_DIM = 128


rope_base = 500000.0
masked_score = -1e30


def rotation_table(positions):
    half = HEAD_DIM // 2
    freqs = rope_base ** (-(jnp.arange(half, dtype=jnp.float32) * 2.0) / HEAD_DIM)
    angles = positions.astype(jnp.float32)[:, None] * freqs[None, :]
    cosine = jnp.concatenate([jnp.cos(angles), jnp.cos(angles)], axis=1)
    sine = jnp.concatenate([jnp.sin(angles), jnp.sin(angles)], axis=1)
    return cosine, sine


def rotate(values, table):
    half = HEAD_DIM // 2
    cosine, sine = table
    count = values.shape[0]
    heads = values.reshape(count, -1, HEAD_DIM)
    turned = jnp.concatenate([-heads[..., half:], heads[..., :half]], axis=-1)
    result = heads * cosine[:, None, :] + turned * sine[:, None, :]
    return result.reshape(count, -1)


def swap_pairs(value, flip):
    count = lax.axis_size("row")
    return lax.ppermute(value, "row", [(r, r ^ flip) for r in range(count)])


def shifted(value, axis, step):
    count = lax.axis_size(axis)
    return lax.ppermute(value, axis, [(i, (i + step) % count) for i in range(count)])


def pick(flag, first, second):
    return jnp.where(flag, first, second)


def on_device(tokens, w_query, w_key, w_value, w_output):
    shard_rows = tokens.shape[0]
    col_count = lax.axis_size("col")
    row_count = lax.axis_size("row")
    seq_count = lax.axis_size("seq")
    block_len = shard_rows * col_count
    key_len = block_len // 2
    seq_at = lax.axis_index("seq")
    row_at = lax.axis_index("row")
    core = row_at % 2
    chip = row_at // 2
    width_q = w_query.shape[1]
    width_kv = w_key.shape[1]
    local_kv = width_kv // HEAD_DIM
    assert row_count == 2 * local_kv
    q_width = width_q // row_count
    score_scale = HEAD_DIM ** (-0.5)

    col_at = lax.axis_index("col")
    pieces = [tokens] + [shifted(tokens, "col", step) for step in range(1, col_count)]
    order = (col_at - jnp.arange(col_count, dtype=jnp.int32)) % col_count
    block_tokens = jnp.take(jnp.stack(pieces), order, axis=0).reshape(block_len, -1)
    part_q = jnp.dot(block_tokens, w_query, preferred_element_type=jnp.float32)
    part_k = jnp.dot(block_tokens, w_key, preferred_element_type=jnp.float32)
    part_v = jnp.dot(block_tokens, w_value, preferred_element_type=jnp.float32)
    q_chunks = part_q.reshape(block_len, row_count, q_width).transpose(1, 0, 2)
    q_chunks = q_chunks.reshape(2, 2, block_len * q_width // HEAD_DIM, HEAD_DIM)

    def kv_chunks(part):
        split = part.reshape(2, key_len, local_kv, HEAD_DIM).transpose(2, 0, 1, 3)
        return split

    chunks = jnp.concatenate([q_chunks, kv_chunks(part_k), kv_chunks(part_v)], axis=2)
    keep_a = lax.dynamic_index_in_dim(chunks, core, axis=1, keepdims=False)
    send_a = lax.dynamic_index_in_dim(chunks, 1 - core, axis=1, keepdims=False)
    summed_a = keep_a + swap_pairs(send_a.astype(jnp.bfloat16), 1).astype(jnp.float32)
    keep_b = lax.dynamic_index_in_dim(summed_a, chip, axis=0, keepdims=False)
    send_b = lax.dynamic_index_in_dim(summed_a, 1 - chip, axis=0, keepdims=False)
    mine = keep_b + swap_pairs(send_b.astype(jnp.bfloat16), 2).astype(jnp.float32)

    q_rows = block_len * q_width // HEAD_DIM
    q_mine = mine[:q_rows].reshape(block_len, q_width)
    k_mine = mine[q_rows : q_rows + key_len]
    v_mine = mine[q_rows + key_len :]

    block_start = seq_at * block_len
    q_pos = block_start + jnp.arange(block_len, dtype=jnp.int32)
    k_offset = core * key_len + jnp.arange(key_len, dtype=jnp.int32)
    q_table = rotation_table(q_pos)
    k_table = tuple(
        lax.dynamic_slice_in_dim(part, core * key_len, key_len, 0) for part in q_table
    )
    query = rotate(q_mine, q_table).astype(jnp.bfloat16)
    keys = rotate(k_mine, k_table).astype(jnp.bfloat16)
    kv_own = jnp.concatenate([keys, v_mine.astype(jnp.bfloat16)], axis=1)

    query_other = swap_pairs(query, 1)
    q_all = jnp.concatenate([query, query_other], axis=1)
    q_heads = q_all.reshape(block_len, -1, HEAD_DIM).transpose(1, 0, 2)
    n_heads = q_heads.shape[0]

    def attend(state, kv_rows, allowed):
        peak, total, summed = state
        key_blk = kv_rows[:, :HEAD_DIM]
        value_blk = kv_rows[:, HEAD_DIM:]
        scores = (
            jnp.einsum("hqd,kd->hqk", q_heads, key_blk, preferred_element_type=jnp.float32)
            * score_scale
        )
        scores = jnp.where(allowed[None], scores, masked_score)
        new_peak = jnp.maximum(peak, jnp.max(scores, axis=-1))
        weights = jnp.exp(scores - new_peak[..., None])
        factor = jnp.exp(peak - new_peak)
        total = total * factor + jnp.sum(weights, axis=-1)
        summed = summed * factor[..., None] + jnp.einsum(
            "hqk,kd->hqd",
            weights.astype(jnp.bfloat16),
            value_blk,
            preferred_element_type=jnp.float32,
        )
        return (new_peak, total, summed)

    state = (
        jnp.full((n_heads, block_len), masked_score, jnp.float32),
        jnp.zeros((n_heads, block_len), jnp.float32),
        jnp.zeros((n_heads, block_len, HEAD_DIM), jnp.float32),
    )
    half = seq_count // 2
    z_at = seq_at % half
    base = seq_at - z_at
    z_fwd = [(s, s - s % half + (s + 1) % half) for s in range(seq_count)]
    z_bwd = [(s, s - s % half + (s - 1) % half) for s in range(seq_count)]
    across = [(s, (s + half) % seq_count) for s in range(seq_count)]
    steps = half // 2
    pending = [(kv_own, seq_at)]
    kv_fwd = kv_own
    kv_bwd = kv_own
    for step in range(1, steps + 2):
        arrived = []
        if step <= steps:
            kv_fwd = lax.ppermute(kv_fwd, "seq", z_fwd)
            arrived.append((kv_fwd, base + (z_at - step) % half))
            if step < steps:
                kv_bwd = lax.ppermute(kv_bwd, "seq", z_bwd)
                arrived.append((kv_bwd, base + (z_at + step) % half))
        got = lax.ppermute(jnp.stack([kv for kv, _ in pending]), "seq", across)
        crossed = [(got[i], (block + half) % seq_count) for i, (_, block) in enumerate(pending)]
        incoming = arrived + crossed
        arrays, state = lax.optimization_barrier(([kv for kv, _ in incoming], state))
        kv_step = jnp.concatenate(arrays, axis=0)
        step_pos = jnp.concatenate([block * block_len + k_offset for _, block in incoming])
        state = attend(state, kv_step, (step_pos < block_start)[None, :])
        pending = arrived

    own_pos = block_start + k_offset
    state = attend(state, kv_own, own_pos[None, :] <= q_pos[:, None])

    peak, total, summed = state
    other_stats, other_norm = swap_pairs(
        (jnp.stack([peak, total]), (summed / total[..., None]).astype(jnp.bfloat16)), 1
    )
    other_peak, other_total = other_stats[0], other_stats[1]
    other_peak, other_total, other_norm = (
        jnp.roll(part, n_heads // 2, axis=0) for part in (other_peak, other_total, other_norm)
    )
    peak_all = jnp.maximum(peak, other_peak)
    factor_a = jnp.exp(peak - peak_all)
    factor_b = jnp.exp(other_peak - peak_all) * other_total
    total_all = total * factor_a + factor_b
    summed_all = summed * factor_a[..., None] + other_norm.astype(jnp.float32) * factor_b[..., None]
    heads_all = (summed_all / total_all[..., None]).astype(jnp.bfloat16)
    own = n_heads // 2
    heads_pair = pick(
        core == 0,
        heads_all,
        jnp.concatenate([heads_all[own:], heads_all[:own]], axis=0),
    )
    heads_pair = heads_pair.reshape(2, own, block_len, HEAD_DIM).transpose(0, 2, 1, 3)
    heads_pair = heads_pair.reshape(2, block_len, q_width)
    got_x = swap_pairs(lax.dynamic_index_in_dim(heads_pair, core, 0, keepdims=False), 2)
    got_partner = swap_pairs(got_x, 1)
    heads_quad_other = jnp.stack(
        [pick(core == 0, got_x, got_partner), pick(core == 0, got_partner, got_x)]
    )
    w_out = w_output.reshape(row_count, q_width, w_output.shape[1])
    w_local = lax.dynamic_slice_in_dim(w_out, 2 * chip, 2, 0)
    w_remote = lax.dynamic_slice_in_dim(w_out, 2 * (1 - chip), 2, 0)
    partial_local = jnp.einsum("rtc,rco->to", heads_pair, w_local, preferred_element_type=jnp.float32)
    partial_remote = jnp.einsum(
        "rtc,rco->to", heads_quad_other, w_remote, preferred_element_type=jnp.float32
    )
    partial_out = (partial_local + partial_remote).astype(jnp.bfloat16)
    out_chunks = partial_out.reshape(col_count, shard_rows, -1)
    result = lax.dynamic_index_in_dim(out_chunks, col_at, 0, keepdims=False).astype(jnp.float32)
    for step in range(1, col_count):
        target = (col_at + step) % col_count
        sent = lax.dynamic_index_in_dim(out_chunks, target, 0, keepdims=False)
        result = result + shifted(sent, "col", step).astype(jnp.float32)
    return result.astype(jnp.bfloat16)


def solution(mesh):
    return jax.shard_map(
        on_device,
        mesh=mesh,
        in_specs=(
            P(("seq", "col"), "row"),
            P("row", "col"),
            P("row", "col"),
            P("row", "col"),
            P("col", "row"),
        ),
        out_specs=P(("seq", "col"), "row"),
        check_vma=False,
    )
```

```python
import jax
import jax.numpy as jnp
from jax import lax
from jax.sharding import PartitionSpec as P

HEADS = 32
KV_HEADS = 8
HEAD_DIM = 128


rope_base = 500000.0
masked_score = -1e30


def rotation_table(positions):
    half = HEAD_DIM // 2
    freqs = rope_base ** (-(jnp.arange(half, dtype=jnp.float32) * 2.0) / HEAD_DIM)
    angles = positions.astype(jnp.float32)[:, None] * freqs[None, :]
    cosine = jnp.concatenate([jnp.cos(angles), jnp.cos(angles)], axis=1)
    sine = jnp.concatenate([jnp.sin(angles), jnp.sin(angles)], axis=1)
    return cosine, sine


def rotate(values, table):
    half = HEAD_DIM // 2
    cosine, sine = table
    count = values.shape[0]
    heads = values.reshape(count, -1, HEAD_DIM)
    turned = jnp.concatenate([-heads[..., half:], heads[..., :half]], axis=-1)
    result = heads * cosine[:, None, :] + turned * sine[:, None, :]
    return result.reshape(count, -1)


def swap_pairs(value, flip):
    count = lax.axis_size("row")
    return lax.ppermute(value, "row", [(r, r ^ flip) for r in range(count)])


def shifted(value, axis, step):
    count = lax.axis_size(axis)
    return lax.ppermute(value, axis, [(i, (i + step) % count) for i in range(count)])


def pick(flag, first, second):
    return jnp.where(flag, first, second)


def on_device(tokens, w_query, w_key, w_value, w_output):
    shard_rows = tokens.shape[0]
    col_count = lax.axis_size("col")
    row_count = lax.axis_size("row")
    seq_count = lax.axis_size("seq")
    block_len = shard_rows * col_count
    key_len = block_len // 2
    seq_at = lax.axis_index("seq")
    row_at = lax.axis_index("row")
    core = row_at % 2
    chip = row_at // 2
    width_q = w_query.shape[1]
    width_kv = w_key.shape[1]
    local_kv = width_kv // HEAD_DIM
    assert row_count == 2 * local_kv
    q_width = width_q // row_count
    score_scale = HEAD_DIM ** (-0.5)

    col_at = lax.axis_index("col")
    pieces = [tokens] + [shifted(tokens, "col", step) for step in range(1, col_count)]
    order = (col_at - jnp.arange(col_count, dtype=jnp.int32)) % col_count
    block_tokens = jnp.take(jnp.stack(pieces), order, axis=0).reshape(block_len, -1)
    part_q = jnp.dot(block_tokens, w_query, preferred_element_type=jnp.float32)
    part_k = jnp.dot(block_tokens, w_key, preferred_element_type=jnp.float32)
    part_v = jnp.dot(block_tokens, w_value, preferred_element_type=jnp.float32)
    q_chunks = part_q.reshape(block_len, row_count, q_width).transpose(1, 0, 2)
    q_chunks = q_chunks.reshape(2, 2, block_len * q_width // HEAD_DIM, HEAD_DIM)

    def kv_chunks(part):
        split = part.reshape(2, key_len, local_kv, HEAD_DIM).transpose(2, 0, 1, 3)
        return split

    chunks = jnp.concatenate([q_chunks, kv_chunks(part_k), kv_chunks(part_v)], axis=2)
    keep_a = lax.dynamic_index_in_dim(chunks, core, axis=1, keepdims=False)
    send_a = lax.dynamic_index_in_dim(chunks, 1 - core, axis=1, keepdims=False)
    summed_a = keep_a + swap_pairs(send_a.astype(jnp.bfloat16), 1).astype(jnp.float32)
    keep_b = lax.dynamic_index_in_dim(summed_a, chip, axis=0, keepdims=False)
    send_b = lax.dynamic_index_in_dim(summed_a, 1 - chip, axis=0, keepdims=False)
    mine = keep_b + swap_pairs(send_b.astype(jnp.bfloat16), 2).astype(jnp.float32)

    q_rows = block_len * q_width // HEAD_DIM
    q_mine = mine[:q_rows].reshape(block_len, q_width)
    k_mine = mine[q_rows : q_rows + key_len]
    v_mine = mine[q_rows + key_len :]

    block_start = seq_at * block_len
    q_pos = block_start + jnp.arange(block_len, dtype=jnp.int32)
    k_offset = core * key_len + jnp.arange(key_len, dtype=jnp.int32)
    q_table = rotation_table(q_pos)
    k_table = tuple(
        lax.dynamic_slice_in_dim(part, core * key_len, key_len, 0) for part in q_table
    )
    query = rotate(q_mine, q_table).astype(jnp.bfloat16)
    keys = rotate(k_mine, k_table).astype(jnp.bfloat16)
    kv_own = jnp.concatenate([keys, v_mine.astype(jnp.bfloat16)], axis=1)

    query_other = swap_pairs(query, 1)
    q_all = jnp.concatenate([query, query_other], axis=1)
    q_heads = q_all.reshape(block_len, -1, HEAD_DIM).transpose(1, 0, 2)
    n_heads = q_heads.shape[0]

    def attend(state, kv_rows, allowed):
        peak, total, summed = state
        key_blk = kv_rows[:, :HEAD_DIM]
        value_blk = kv_rows[:, HEAD_DIM:]
        scores = (
            jnp.einsum("hqd,kd->hqk", q_heads, key_blk, preferred_element_type=jnp.float32)
            * score_scale
        )
        scores = jnp.where(allowed[None], scores, masked_score)
        new_peak = jnp.maximum(peak, jnp.max(scores, axis=-1))
        weights = jnp.exp(scores - new_peak[..., None])
        factor = jnp.exp(peak - new_peak)
        total = total * factor + jnp.sum(weights, axis=-1)
        summed = summed * factor[..., None] + jnp.einsum(
            "hqk,kd->hqd",
            weights.astype(jnp.bfloat16),
            value_blk,
            preferred_element_type=jnp.float32,
        )
        return (new_peak, total, summed)

    state = (
        jnp.full((n_heads, block_len), masked_score, jnp.float32),
        jnp.zeros((n_heads, block_len), jnp.float32),
        jnp.zeros((n_heads, block_len, HEAD_DIM), jnp.float32),
    )
    half = seq_count // 2
    z_at = seq_at % half
    base = seq_at - z_at
    z_fwd = [(s, s - s % half + (s + 1) % half) for s in range(seq_count)]
    z_bwd = [(s, s - s % half + (s - 1) % half) for s in range(seq_count)]
    across = [(s, (s + half) % seq_count) for s in range(seq_count)]
    steps = half // 2
    pending = [(kv_own, seq_at)]
    kv_fwd = kv_own
    kv_bwd = kv_own
    for step in range(1, steps + 2):
        arrived = []
        if step <= steps:
            kv_fwd = lax.ppermute(kv_fwd, "seq", z_fwd)
            arrived.append((kv_fwd, base + (z_at - step) % half))
            if step < steps:
                kv_bwd = lax.ppermute(kv_bwd, "seq", z_bwd)
                arrived.append((kv_bwd, base + (z_at + step) % half))
        got = lax.ppermute(jnp.stack([kv for kv, _ in pending]), "seq", across)
        crossed = [(got[i], (block + half) % seq_count) for i, (_, block) in enumerate(pending)]
        incoming = arrived + crossed
        arrays = [kv for kv, _ in incoming]
        if step <= steps:
            arrays, state = lax.optimization_barrier((arrays, state))
        kv_step = jnp.concatenate(arrays, axis=0)
        step_pos = jnp.concatenate([block * block_len + k_offset for _, block in incoming])
        state = attend(state, kv_step, (step_pos < block_start)[None, :])
        pending = arrived

    own_pos = block_start + k_offset
    state = attend(state, kv_own, own_pos[None, :] <= q_pos[:, None])

    peak, total, summed = state
    other_peak, other_total, other_norm = swap_pairs(
        (peak, total, (summed / total[..., None]).astype(jnp.bfloat16)), 1
    )
    other_peak, other_total, other_norm = (
        jnp.roll(part, n_heads // 2, axis=0) for part in (other_peak, other_total, other_norm)
    )
    peak_all = jnp.maximum(peak, other_peak)
    factor_a = jnp.exp(peak - peak_all)
    factor_b = jnp.exp(other_peak - peak_all) * other_total
    total_all = total * factor_a + factor_b
    summed_all = summed * factor_a[..., None] + other_norm.astype(jnp.float32) * factor_b[..., None]
    heads_all = (summed_all / total_all[..., None]).astype(jnp.bfloat16)
    own = n_heads // 2
    heads_pair = pick(
        core == 0,
        heads_all,
        jnp.concatenate([heads_all[own:], heads_all[:own]], axis=0),
    )
    heads_pair = heads_pair.reshape(2, own, block_len, HEAD_DIM).transpose(0, 2, 1, 3)
    heads_pair = heads_pair.reshape(2, block_len, q_width)
    got_x = swap_pairs(lax.dynamic_index_in_dim(heads_pair, core, 0, keepdims=False), 2)
    got_partner = swap_pairs(got_x, 1)
    heads_quad_other = jnp.stack(
        [pick(core == 0, got_x, got_partner), pick(core == 0, got_partner, got_x)]
    )
    w_out = w_output.reshape(row_count, q_width, w_output.shape[1])
    w_local = lax.dynamic_slice_in_dim(w_out, 2 * chip, 2, 0)
    w_remote = lax.dynamic_slice_in_dim(w_out, 2 * (1 - chip), 2, 0)
    partial_local = jnp.einsum("rtc,rco->to", heads_pair, w_local, preferred_element_type=jnp.float32)
    partial_remote = jnp.einsum(
        "rtc,rco->to", heads_quad_other, w_remote, preferred_element_type=jnp.float32
    )
    partial_out = (partial_local + partial_remote).astype(jnp.bfloat16)
    out_chunks = partial_out.reshape(col_count, shard_rows, -1)
    result = lax.dynamic_index_in_dim(out_chunks, col_at, 0, keepdims=False).astype(jnp.float32)
    for step in range(1, col_count):
        target = (col_at + step) % col_count
        sent = lax.dynamic_index_in_dim(out_chunks, target, 0, keepdims=False)
        result = result + shifted(sent, "col", step).astype(jnp.float32)
    return result.astype(jnp.bfloat16)


def solution(mesh):
    return jax.shard_map(
        on_device,
        mesh=mesh,
        in_specs=(
            P(("seq", "col"), "row"),
            P("row", "col"),
            P("row", "col"),
            P("row", "col"),
            P("col", "row"),
        ),
        out_specs=P(("seq", "col"), "row"),
        check_vma=False,
    )
```
